512 devices in a mesh: depth: 128 (over z, x, core), dp: 4 (over y).
Axes of the slice: x: 4, y: 4, z: 16, core: 2. Of those that a mesh axis runs over, the one named last changes fastest.
Arguments:
- cpoints: float32 [128, 4, 64, 256], P('depth', 'dp'), may hold values from -6 to 6, as said below
- weights: bfloat16 [512, 64, 576], P('depth'), may hold values from -12 to 12
- coarse_gain: float32 [128, 64], P('depth'), may hold values from 0.04 to 1
- cotangent: float32 [128, 4, 64, 256], P('depth', 'dp'), may hold values from -0.6 to 0.6
Outputs:
- corrected: float32 [128, 4, 64, 256], P('depth', 'dp')
- grad_cpoints: float32 [128, 4, 64, 256], P('depth', 'dp')
- grad_weights: float32 [512, 64, 576], P('depth')
The draws below stay inside these ranges and needn't reach their ends.
Inputs may be any that keep to these rules, and one draw needn't show every extreme that they name: cpoints[0] holds the network input; cpoints[d] the current guess of the state entering block d.
All inputs are finite; a program needn't handle non-finite values.
Results may differ from the reference program's by a relative error of at most 0.0041.
Values sent between devices are 32-bit elements; how exact they have to be, the bound alone decides.
No kernel may reach another device: no remote copies, remote signals or barrier semaphores. Data moves between devices by JAX's collectives and lax.ppermute only.
A program may use at most 64 MiB of HBM per device.

```python
import math
import jax
import jax.numpy as jnp
from jax import lax

CHANNEL_COUNT = 64
LAYERS_DEV = 4
WID = 16
PIXELS = 256
LAYER_BLOCKS = 128
LAYERS = 512
IMAGES = 4


def draw_cpoints(key, part):
    shape_all = (LAYER_BLOCKS, IMAGES, CHANNEL_COUNT, PIXELS)
    first_key = jax.random.fold_in(key, 0)
    leading = jnp.arange(LAYER_BLOCKS)[:, None, None, None] == 0
    base = jnp.clip(jax.random.normal(first_key, shape_all, jnp.float32), -6.0, 6.0)
    return jnp.where(leading, base, 0.5 * base)


def draw_coarse_gain(key, part):
    random_split_keys = jax.random.split(key, 6)
    slow_share = 0.5
    chooser = jax.random.uniform(random_split_keys[0], (1, CHANNEL_COUNT), jnp.float32)
    slow_scale = jax.random.uniform(random_split_keys[1], (1, CHANNEL_COUNT), jnp.float32, 0.1, 0.4)
    fast_scale = jax.random.uniform(random_split_keys[2], (1, CHANNEL_COUNT), jnp.float32, 0.3, 1.5)
    factor = jnp.exp(jax.random.uniform(random_split_keys[3], (LAYER_BLOCKS, CHANNEL_COUNT), jnp.float32, -0.7, 0.7))
    coarse_rate = jnp.exp(math.log(0.1) * slow_scale * factor / LAYER_BLOCKS)
    fast_rate = jnp.exp(-fast_scale * factor)
    relaxation_sweep = jax.random.uniform(random_split_keys[4], (LAYER_BLOCKS, 1), jnp.float32) < 3.0 / LAYER_BLOCKS
    sweep_boundary = jax.random.uniform(random_split_keys[5], (LAYER_BLOCKS, CHANNEL_COUNT), jnp.float32, 0.5, 0.8)
    coarse_rate = jnp.where(relaxation_sweep, coarse_rate * sweep_boundary, coarse_rate)
    return jnp.where(chooser < slow_share, coarse_rate, fast_rate)


def shard_levels(own_key, shape, cuts, smallest, top_value):
    factor_of, own = 1.0, jax.random.fold_in(own_key, 6)
    for position, shards_of in cuts:
        draws = jnp.exp(jax.random.uniform(jax.random.fold_in(own, position), (shards_of,), jnp.float32, smallest / len(cuts), top_value / len(cuts)))
        factor_of = factor_of * jnp.repeat(draws, shape[position] // shards_of).reshape([-1 if axis == position else 1 for axis in range(len(shape))])
    return factor_of


def scatter_about(rng, dims, scale, limit, shards=(), dtype=jnp.bfloat16):
    result = scale * jax.random.normal(rng, dims, jnp.float32)
    if shards:
        result = result * shard_levels(rng, dims, shards, -0.22, 0.18)
    return jnp.clip(result, -limit, limit).astype(dtype)


def setup_inputs(seed: int = 0) -> dict:
    seeds = jax.random.split(jax.random.key(seed), 5)
    return {
        "cpoints": draw_cpoints(jax.random.fold_in(seeds[4], 71), 0),
        "weights": scatter_about(seeds[1], (LAYERS, CHANNEL_COUNT, 9 * CHANNEL_COUNT), (LAYERS * (900 * CHANNEL_COUNT) ** -0.5), 12.0, ((0, 128),)),
        "coarse_gain": draw_coarse_gain(jax.random.fold_in(seeds[4], 71), 0),
        "cotangent": scatter_about(seeds[3], (LAYER_BLOCKS, IMAGES, CHANNEL_COUNT, PIXELS), 0.1, 0.6, ((0, 128), (1, 4)), jnp.float32),
    }


TAP_OFFSETS = [(-1, -1), (-1, 0), (-1, 1), (0, -1), (0, 0), (0, 1), (1, -1), (1, 0), (1, 1)]


def shift_pixels(values, shift_down, shift_right, row_width):
    pixel_count = values.shape[-1]
    offset = shift_down * row_width + shift_right
    padded = jnp.pad(values, [(0, 0)] * (values.ndim - 1) + [(row_width + 1, row_width + 1)])
    shifted = lax.slice_in_dim(padded, row_width + 1 + offset, row_width + 1 + offset + pixel_count, axis=values.ndim - 1)
    column = jnp.arange(pixel_count) % row_width + shift_right
    inside = (column >= 0) & (column < row_width)
    return jnp.where(inside, shifted, jnp.zeros_like(shifted))


def unfold(values, row_width):
    return jnp.concatenate([shift_pixels(values, a, b, row_width) for a, b in TAP_OFFSETS], axis=1)


def fold_taps(tap_grads, row_width):
    channels = tap_grads.shape[1] // 9
    accumulated = jnp.zeros((tap_grads.shape[0], channels, tap_grads.shape[2]), jnp.float32)
    for tap_index, (a, b) in enumerate(TAP_OFFSETS):
        piece = tap_grads[:, tap_index * channels:(tap_index + 1) * channels]
        accumulated = accumulated + shift_pixels(piece, -a, -b, row_width)
    return accumulated


def layer_forward(current, weight, step_size):
    squashed = jnp.tanh(current)
    patches = unfold(squashed.astype(jnp.bfloat16), WID)
    mixed = jnp.einsum("ok,bkp->bop", weight.astype(jnp.float32), patches.astype(jnp.float32))
    return current + step_size * mixed


def forward_block_pass(current, block_weights, step_size):
    for layer in range(LAYERS_DEV):
        current = layer_forward(current, block_weights[layer], step_size)
    return current


def block_backward(current, block_weights, upstream, step_size):
    inputs_kept = []
    for layer in range(LAYERS_DEV):
        inputs_kept.append(current)
        current = layer_forward(current, block_weights[layer], step_size)
    layer_grads = [None] * LAYERS_DEV
    for layer in reversed(range(LAYERS_DEV)):
        squashed = jnp.tanh(inputs_kept[layer])
        patches = unfold(squashed.astype(jnp.bfloat16), WID).astype(jnp.float32)
        scaled = (step_size * upstream).astype(jnp.bfloat16).astype(jnp.float32)
        layer_grads[layer] = jnp.einsum("bop,bkp->ok", scaled, patches)
        spread = jnp.einsum("ok,bop->bkp", block_weights[layer].astype(jnp.float32), scaled)
        upstream = upstream + (1.0 - squashed * squashed) * fold_taps(spread, WID)
    return upstream, jnp.stack(layer_grads)


def reference(cpoints, weights, coarse_gain, cotangent):
    step_size = 1.0 / LAYERS
    blocks = weights.reshape(LAYER_BLOCKS, LAYERS_DEV, CHANNEL_COUNT, 9 * CHANNEL_COUNT)
    relaxed = lax.map(lambda inputs_pair: forward_block_pass(inputs_pair[0], inputs_pair[1], step_size), (cpoints, blocks))
    start_state = jnp.concatenate([cpoints[:1], relaxed[:-1]], axis=0)
    propagated = lax.map(lambda inputs_pair: forward_block_pass(inputs_pair[0], inputs_pair[1], step_size), (start_state, blocks))
    first_block = (jnp.arange(LAYER_BLOCKS) == 0)[:, None, None, None]
    gained_start = coarse_gain[:, None, :, None] * start_state
    offset = propagated - jnp.where(first_block, jnp.zeros_like(gained_start), gained_start)

    def forward_step(carried_in, inputs_pair):
        rate_vec, increment = inputs_pair
        leaving = rate_vec[None, :, None] * carried_in + increment
        return leaving, leaving

    _, corrected = lax.scan(forward_step, jnp.zeros_like(offset[0]), (coarse_gain, offset))

    def adjoint_step(carried_in, inputs_pair):
        rate_vec, incoming = inputs_pair
        adjoint_here = incoming + carried_in
        return rate_vec[None, :, None] * adjoint_here, (adjoint_here, carried_in)

    _, (adjoints, passed_back) = lax.scan(adjoint_step, jnp.zeros_like(cotangent[0]), (coarse_gain, cotangent), reverse=True)
    back_start, start_grads = lax.map(lambda inputs_trio: block_backward(inputs_trio[0], inputs_trio[1], inputs_trio[2], step_size), (start_state, blocks, adjoints))
    successor_block = jnp.concatenate([back_start[1:], jnp.zeros_like(back_start[:1])], axis=0)
    relaxed_bar = successor_block - passed_back
    back_own, own_grads = lax.map(lambda inputs_trio: block_backward(inputs_trio[0], inputs_trio[1], inputs_trio[2], step_size), (cpoints, blocks, relaxed_bar))
    grad_cpoints = back_own.at[0].add(back_start[0])
    grad_weights = (start_grads + own_grads).reshape(LAYERS, CHANNEL_COUNT, 9 * CHANNEL_COUNT)
    return (corrected, grad_cpoints, grad_weights)
```

```python
import jax
import jax.numpy as jnp
from jax import lax
from jax.sharding import PartitionSpec as P

WID = 16


TAP_OFFSETS = [(-1, -1), (-1, 0), (-1, 1), (0, -1), (0, 0), (0, 1), (1, -1), (1, 0), (1, 1)]


def pack(gain, state):
    row = jnp.pad(gain, (0, state.shape[-1] - gain.shape[0]))
    return jnp.concatenate([state.reshape(-1, state.shape[-1]), row[None]], axis=0)


def scan_along(gain, state, axis, reverse):
    count = lax.axis_size(axis)
    rows = state.shape[-2]
    carried = jnp.zeros_like(state)
    total = state
    distance = 1
    while distance < count:
        final = 2 * distance >= count
        step = -distance if reverse else distance
        message = total if final else pack(gain, total)
        arrived = passed_along(message, axis, step)
        if final:
            part = arrived
        else:
            part = arrived[:rows].reshape(state.shape)
        carried = carried + gain[:, None] * part
        total = state + carried
        if not final:
            gain = gain * arrived[rows, : gain.shape[0]]
        distance *= 2
    return total, carried


def passed_along(block, axis, distance):
    devices = range(lax.axis_size(axis))
    route = [(i - distance, i) for i in devices if i - distance in devices]
    return lax.ppermute(block, axis, route)


def shift_pixels(values, shift_down, shift_right, row_width):
    pixel_count = values.shape[-1]
    offset = shift_down * row_width + shift_right
    padded = jnp.pad(values, [(0, 0)] * (values.ndim - 1) + [(row_width + 1, row_width + 1)])
    shifted = lax.slice_in_dim(
        padded, row_width + 1 + offset, row_width + 1 + offset + pixel_count, axis=values.ndim - 1
    )
    column = jnp.arange(pixel_count) % row_width + shift_right
    inside = (column >= 0) & (column < row_width)
    return jnp.where(inside, shifted, jnp.zeros_like(shifted))


def unfold(values, row_width):
    return jnp.concatenate([shift_pixels(values, a, b, row_width) for a, b in TAP_OFFSETS], axis=1)


def fold_taps(tap_grads, row_width):
    channels = tap_grads.shape[1] // 9
    accumulated = jnp.zeros((tap_grads.shape[0], channels, tap_grads.shape[2]), jnp.float32)
    for tap_index, (a, b) in enumerate(TAP_OFFSETS):
        piece = tap_grads[:, tap_index * channels : (tap_index + 1) * channels]
        accumulated = accumulated + shift_pixels(piece, -a, -b, row_width)
    return accumulated


def run_block(current, block_weights, step_size):
    inputs_kept = []
    for layer in range(block_weights.shape[0]):
        inputs_kept.append(current)
        squashed = jnp.tanh(current)
        patches = unfold(squashed.astype(jnp.bfloat16), WID)
        mixed = jnp.einsum(
            "ok,bkp->bop", block_weights[layer], patches, preferred_element_type=jnp.float32
        )
        current = current + step_size * mixed
    return (current, inputs_kept)


def back_block(inputs_kept, block_weights, upstream, step_size):
    layer_count = block_weights.shape[0]
    layer_grads = [None] * layer_count
    for layer in reversed(range(layer_count)):
        squashed = jnp.tanh(inputs_kept[layer])
        patches = unfold(squashed.astype(jnp.bfloat16), WID)
        scaled = (step_size * upstream).astype(jnp.bfloat16)
        layer_grads[layer] = jnp.einsum(
            "bop,bkp->ok", scaled, patches, preferred_element_type=jnp.float32
        )
        spread = jnp.einsum(
            "ok,bop->bkp", block_weights[layer], scaled, preferred_element_type=jnp.float32
        )
        upstream = upstream + (1.0 - squashed * squashed) * fold_taps(spread, WID)
    return (upstream, jnp.stack(layer_grads))


def body(cpoints, weights, coarse_gain, cotangent):
    step_size = 1.0 / (weights.shape[0] * lax.axis_size("depth"))
    own_state = cpoints[0]
    rate_vec = coarse_gain[0]
    cot_here = cotangent[0]
    leading = lax.axis_index("depth") == 0
    next_rate = passed_along(rate_vec, "depth", -1)
    adjoint_here, passed_in = scan_along(next_rate, cot_here, "depth", True)
    relaxed, own_kept = run_block(own_state, weights, step_size)
    arriving = passed_along(relaxed, "depth", 1)
    start_state = jnp.where(leading, own_state, arriving)
    propagated, start_kept = run_block(start_state, weights, step_size)
    gained_start = rate_vec[None, :, None] * start_state
    offset = propagated - jnp.where(leading, jnp.zeros_like(gained_start), gained_start)
    corrected, _ = scan_along(rate_vec, offset, "depth", False)
    back_start, start_grads = back_block(start_kept, weights, adjoint_here, step_size)
    arriving_bar = passed_along(back_start, "depth", -1)
    relaxed_bar = arriving_bar - passed_in
    back_own, own_grads = back_block(own_kept, weights, relaxed_bar, step_size)
    grad_cpoints = jnp.where(leading, back_own + back_start, back_own)
    grad_weights = lax.psum(start_grads + own_grads, "dp")
    return (corrected[None], grad_cpoints[None], grad_weights)


def solution(mesh):
    placed = (
        P("depth", "dp", None, None),
        P("depth", None, None),
        P("depth", None),
        P("depth", "dp", None, None),
    )
    return jax.shard_map(
        body,
        mesh=mesh,
        in_specs=placed,
        out_specs=(
            P("depth", "dp", None, None),
            P("depth", "dp", None, None),
            P("depth", None, None),
        ),
        check_vma=False,
    )
```

```python
import jax
import jax.numpy as jnp
from jax import lax
from jax.sharding import PartitionSpec as P

WID = 16


TAP_OFFSETS = [(-1, -1), (-1, 0), (-1, 1), (0, -1), (0, 0), (0, 1), (1, -1), (1, 0), (1, 1)]


def pack(gain, state):
    row = jnp.pad(gain, (0, state.shape[-1] - gain.shape[0]))
    return jnp.concatenate([state.reshape(-1, state.shape[-1]), row[None]], axis=0)


def exchange(gain, state, axis, bit):
    count = lax.axis_size(axis)
    arrived = lax.ppermute(pack(gain, state), axis, [(i, i ^ (1 << bit)) for i in range(count)])
    rows = state.shape[-2]
    return arrived[rows, : gain.shape[0]], arrived[:rows].reshape(state.shape)


def scan_round(scan, arrived, partner_first, bit, last):
    part_gain, part_state, whole_gain, whole_state = scan
    got_gain, got_state = arrived
    take = partner_first(bit)
    part_state = jnp.where(take, part_state + part_gain[:, None] * got_state, part_state)
    part_gain = jnp.where(take, part_gain * got_gain, part_gain)
    if not last:
        whole_state = jnp.where(
            take,
            whole_state + whole_gain[:, None] * got_state,
            got_state + got_gain[:, None] * whole_state,
        )
        whole_gain = whole_gain * got_gain
    return (part_gain, part_state, whole_gain, whole_state)


def dp_sum(terms, axis):
    count = lax.axis_size(axis)
    if count != 4:
        return lax.psum(terms, axis)
    got = [lax.ppermute(terms, axis, [(i, i ^ k) for i in range(count)]) for k in (1, 2, 3)]
    return (terms + got[0]) + (got[1] + got[2])


def passed_along(block, axis, distance):
    devices = range(lax.axis_size(axis))
    route = [(i - distance, i) for i in devices if i - distance in devices]
    return lax.ppermute(block, axis, route)


def shift_pixels(values, shift_down, shift_right, row_width):
    pixel_count = values.shape[-1]
    offset = shift_down * row_width + shift_right
    padded = jnp.pad(values, [(0, 0)] * (values.ndim - 1) + [(row_width + 1, row_width + 1)])
    shifted = lax.slice_in_dim(
        padded, row_width + 1 + offset, row_width + 1 + offset + pixel_count, axis=values.ndim - 1
    )
    column = jnp.arange(pixel_count) % row_width + shift_right
    inside = (column >= 0) & (column < row_width)
    return jnp.where(inside, shifted, jnp.zeros_like(shifted))


def unfold(values, row_width):
    return jnp.concatenate([shift_pixels(values, a, b, row_width) for a, b in TAP_OFFSETS], axis=1)


def fold_taps(tap_grads, row_width):
    channels = tap_grads.shape[1] // 9
    accumulated = jnp.zeros((tap_grads.shape[0], channels, tap_grads.shape[2]), jnp.float32)
    for tap_index, (a, b) in enumerate(TAP_OFFSETS):
        piece = tap_grads[:, tap_index * channels : (tap_index + 1) * channels]
        accumulated = accumulated + shift_pixels(piece, -a, -b, row_width)
    return accumulated


def run_block(current, block_weights, step_size):
    inputs_kept = []
    for layer in range(block_weights.shape[0]):
        inputs_kept.append(current)
        squashed = jnp.tanh(current)
        patches = unfold(squashed.astype(jnp.bfloat16), WID)
        mixed = jnp.einsum(
            "ok,bkp->bop", block_weights[layer], patches, preferred_element_type=jnp.float32
        )
        current = current + step_size * mixed
    return (current, inputs_kept)


def back_block(inputs_kept, block_weights, upstream, step_size):
    layer_count = block_weights.shape[0]
    layer_grads = [None] * layer_count
    for layer in reversed(range(layer_count)):
        squashed = jnp.tanh(inputs_kept[layer])
        patches = unfold(squashed.astype(jnp.bfloat16), WID)
        scaled = (step_size * upstream).astype(jnp.bfloat16)
        layer_grads[layer] = jnp.einsum(
            "bop,bkp->ok", scaled, patches, preferred_element_type=jnp.float32
        )
        spread = jnp.einsum(
            "ok,bop->bkp", block_weights[layer], scaled, preferred_element_type=jnp.float32
        )
        upstream = upstream + (1.0 - squashed * squashed) * fold_taps(spread, WID)
    return (upstream, jnp.stack(layer_grads))


def body(cpoints, weights, coarse_gain, cotangent):
    step_size = 1.0 / (weights.shape[0] * lax.axis_size("depth"))
    rounds = (lax.axis_size("depth") - 1).bit_length()
    place = lax.axis_index("depth")
    own_state = cpoints[0]
    rate_vec = coarse_gain[0]
    cot_here = cotangent[0]
    leading = place == 0

    def before(bit):
        return (place >> bit) % 2 == 1

    def after(bit):
        return (place >> bit) % 2 == 0

    reverse = (jnp.ones_like(rate_vec), jnp.zeros_like(cot_here), rate_vec, rate_vec[None, :, None] * cot_here)
    lag = min(3, rounds - 1)
    for bit in range(lag):
        reverse = scan_round(reverse, exchange(reverse[2], reverse[3], "depth", bit), after, bit, bit == rounds - 1)
    relaxed, own_kept = run_block(own_state, weights, step_size)
    arriving = passed_along(relaxed, "depth", 1)
    start_state = jnp.where(leading, own_state, arriving)
    propagated, start_kept = run_block(start_state, weights, step_size)
    gained_start = rate_vec[None, :, None] * start_state
    offset = propagated - jnp.where(leading, jnp.zeros_like(gained_start), gained_start)
    forward = (rate_vec, offset, rate_vec, offset)
    for bit in range(rounds):
        rbit = bit + lag
        if rbit < rounds:
            reverse, forward = lax.optimization_barrier((reverse, forward))
            got_r = exchange(reverse[2], reverse[3], "depth", rbit)
            got_f = exchange(forward[2], forward[3], "depth", bit)
            reverse = scan_round(reverse, got_r, after, rbit, rbit == rounds - 1)
        else:
            got_f = exchange(forward[2], forward[3], "depth", bit)
        forward = scan_round(forward, got_f, before, bit, bit == rounds - 1)
        if rbit == rounds - 1:
            passed_in = reverse[1]
            adjoint_here = cot_here + passed_in
            back_start, start_grads = back_block(start_kept, weights, adjoint_here, step_size)
            start_sum = dp_sum(start_grads, "dp")
            arriving_bar = passed_along(back_start, "depth", -1)
            relaxed_bar = arriving_bar - passed_in
            back_own, own_grads = back_block(own_kept, weights, relaxed_bar, step_size)
    corrected = forward[1]
    grad_cpoints = jnp.where(leading, back_own + back_start, back_own)
    grad_weights = start_sum + dp_sum(own_grads, "dp")
    return (corrected[None], grad_cpoints[None], grad_weights)


def solution(mesh):
    placed = (
        P("depth", "dp", None, None),
        P("depth", None, None),
        P("depth", None),
        P("depth", "dp", None, None),
    )
    return jax.shard_map(
        body,
        mesh=mesh,
        in_specs=placed,
        out_specs=(
            P("depth", "dp", None, None),
            P("depth", "dp", None, None),
            P("depth", None, None),
        ),
        check_vma=False,
    )
```

```python
import jax
import jax.numpy as jnp
from jax import lax
from jax.sharding import PartitionSpec as P

WID = 16


TAP_OFFSETS = [(-1, -1), (-1, 0), (-1, 1), (0, -1), (0, 0), (0, 1), (1, -1), (1, 0), (1, 1)]


def pack(gain, state):
    row = jnp.pad(gain, (0, state.shape[-1] - gain.shape[0]))
    return jnp.concatenate([state.reshape(-1, state.shape[-1]), row[None]], axis=0)


def exchange(gain, state, axis, bit):
    count = lax.axis_size(axis)
    arrived = lax.ppermute(pack(gain, state), axis, [(i, i ^ (1 << bit)) for i in range(count)])
    rows = state.size // state.shape[-1]
    return arrived[rows, : gain.shape[0]], arrived[:rows].reshape(state.shape)


def scan_round(scan, arrived, partner_first, bit, last):
    part_gain, part_state, whole_gain, whole_state = scan
    got_gain, got_state = arrived
    take = partner_first(bit)
    part_state = jnp.where(take, part_state + part_gain[:, None] * got_state, part_state)
    part_gain = jnp.where(take, part_gain * got_gain, part_gain)
    if not last:
        whole_state = jnp.where(
            take,
            whole_state + whole_gain[:, None] * got_state,
            got_state + got_gain[:, None] * whole_state,
        )
        whole_gain = whole_gain * got_gain
    return (part_gain, part_state, whole_gain, whole_state)


def gather_images(block, axis):
    count = lax.axis_size(axis)
    got = [lax.ppermute(block, axis, [(i, i ^ k) for i in range(count)]) for k in range(1, count)]
    return jnp.stack([block] + got)


def symmetric_sum(slots):
    while slots.shape[0] > 1:
        slots = slots[0::2] + slots[1::2]
    return slots[0]


def passed_along(block, axis, distance):
    devices = range(lax.axis_size(axis))
    route = [(i - distance, i) for i in devices if i - distance in devices]
    return lax.ppermute(block, axis, route)


def shift_pixels(values, shift_down, shift_right, row_width):
    pixel_count = values.shape[-1]
    offset = shift_down * row_width + shift_right
    padded = jnp.pad(values, [(0, 0)] * (values.ndim - 1) + [(row_width + 1, row_width + 1)])
    shifted = lax.slice_in_dim(
        padded, row_width + 1 + offset, row_width + 1 + offset + pixel_count, axis=values.ndim - 1
    )
    column = jnp.arange(pixel_count) % row_width + shift_right
    inside = (column >= 0) & (column < row_width)
    return jnp.where(inside, shifted, jnp.zeros_like(shifted))


def unfold(values, row_width):
    return jnp.concatenate([shift_pixels(values, a, b, row_width) for a, b in TAP_OFFSETS], axis=1)


def fold_taps(tap_grads, row_width):
    channels = tap_grads.shape[1] // 9
    accumulated = jnp.zeros((tap_grads.shape[0], channels, tap_grads.shape[2]), jnp.float32)
    for tap_index, (a, b) in enumerate(TAP_OFFSETS):
        piece = tap_grads[:, tap_index * channels : (tap_index + 1) * channels]
        accumulated = accumulated + shift_pixels(piece, -a, -b, row_width)
    return accumulated


def run_block(current, block_weights, step_size):
    inputs_kept = []
    for layer in range(block_weights.shape[0]):
        inputs_kept.append(current)
        squashed = jnp.tanh(current)
        patches = unfold(squashed.astype(jnp.bfloat16), WID)
        mixed = jnp.einsum(
            "ok,bkp->bop", block_weights[layer], patches, preferred_element_type=jnp.float32
        )
        current = current + step_size * mixed
    return (current, inputs_kept)


def back_block(inputs_kept, block_weights, upstream, step_size):
    layer_count = block_weights.shape[0]
    layer_grads = [None] * layer_count
    for layer in reversed(range(layer_count)):
        squashed = jnp.tanh(inputs_kept[layer])
        patches = unfold(squashed.astype(jnp.bfloat16), WID)
        scaled = (step_size * upstream).astype(jnp.bfloat16)
        layer_grads[layer] = jnp.einsum(
            "bop,bkp->bok", scaled, patches, preferred_element_type=jnp.float32
        )
        spread = jnp.einsum(
            "ok,bop->bkp", block_weights[layer], scaled, preferred_element_type=jnp.float32
        )
        upstream = upstream + (1.0 - squashed * squashed) * fold_taps(spread, WID)
    return (upstream, jnp.stack(layer_grads, axis=1))


def body(cpoints, weights, coarse_gain, cotangent):
    step_size = 1.0 / (weights.shape[0] * lax.axis_size("depth"))
    rounds = (lax.axis_size("depth") - 1).bit_length()
    place = lax.axis_index("depth")
    images = gather_images(jnp.stack([cpoints[0, 0], cotangent[0, 0]]), "dp")
    own_state = images[:, 0]
    rate_vec = coarse_gain[0]
    cot_here = images[:, 1]
    leading = place == 0

    def before(bit):
        return (place >> bit) % 2 == 1

    def after(bit):
        return (place >> bit) % 2 == 0

    reverse = (jnp.ones_like(rate_vec), jnp.zeros_like(cot_here), rate_vec, rate_vec[None, :, None] * cot_here)
    lag = min(3, rounds - 1)
    for bit in range(lag):
        reverse = scan_round(reverse, exchange(reverse[2], reverse[3], "depth", bit), after, bit, bit == rounds - 1)
    relaxed, own_kept = run_block(own_state, weights, step_size)
    arriving = passed_along(relaxed, "depth", 1)
    start_state = jnp.where(leading, own_state, arriving)
    propagated, start_kept = run_block(start_state, weights, step_size)
    gained_start = rate_vec[None, :, None] * start_state
    offset = propagated - jnp.where(leading, jnp.zeros_like(gained_start), gained_start)
    forward = (rate_vec, offset, rate_vec, offset)
    for bit in range(rounds):
        rbit = bit + lag
        if rbit < rounds:
            reverse, forward = lax.optimization_barrier((reverse, forward))
            got_r = exchange(reverse[2], reverse[3], "depth", rbit)
            got_f = exchange(forward[2], forward[3], "depth", bit)
            reverse = scan_round(reverse, got_r, after, rbit, rbit == rounds - 1)
        else:
            got_f = exchange(forward[2], forward[3], "depth", bit)
        forward = scan_round(forward, got_f, before, bit, bit == rounds - 1)
        if rbit == rounds - 1:
            passed_in = reverse[1]
            adjoint_here = cot_here + passed_in
            back_start, start_grads = back_block(start_kept, weights, adjoint_here, step_size)
            arriving_bar = passed_along(back_start, "depth", -1)
            relaxed_bar = arriving_bar - passed_in
            back_own, own_grads = back_block(own_kept, weights, relaxed_bar, step_size)
    corrected = forward[1][:1]
    grad_cpoints = jnp.where(leading, back_own[:1] + back_start[:1], back_own[:1])
    grad_weights = symmetric_sum(start_grads + own_grads)
    return (corrected[None], grad_cpoints[None], grad_weights)


def solution(mesh):
    placed = (
        P("depth", "dp", None, None),
        P("depth", None, None),
        P("depth", None),
        P("depth", "dp", None, None),
    )
    return jax.shard_map(
        body,
        mesh=mesh,
        in_specs=placed,
        out_specs=(
            P("depth", "dp", None, None),
            P("depth", "dp", None, None),
            P("depth", None, None),
        ),
        check_vma=False,
    )
```

```python
import jax
import jax.numpy as jnp
from jax import lax
from jax.sharding import PartitionSpec as P

WID = 16


TAP_OFFSETS = [(-1, -1), (-1, 0), (-1, 1), (0, -1), (0, 0), (0, 1), (1, -1), (1, 0), (1, 1)]


def pack(gains, states):
    width = states.shape[-1]
    rows = [jnp.pad(g, (0, width - g.shape[0]))[None] for g in gains]
    return jnp.concatenate([states.reshape(-1, width)] + rows, axis=0)


def exchange(gains, states, axis, bit):
    count = lax.axis_size(axis)
    arrived = lax.ppermute(pack(gains, states), axis, [(i, i ^ (1 << bit)) for i in range(count)])
    rows = states.size // states.shape[-1]
    each = states.shape[1:]
    got = arrived[:rows].reshape(states.shape)
    return tuple(
        (arrived[rows + k, : g.shape[0]], got[k].reshape(each)) for k, g in enumerate(gains)
    )


def scan_round(scan, arrived, partner_first, bit, last):
    part_gain, part_state, whole_gain, whole_state = scan
    got_gain, got_state = arrived
    take = partner_first(bit)
    part_state = jnp.where(take, part_state + part_gain[:, None] * got_state, part_state)
    part_gain = jnp.where(take, part_gain * got_gain, part_gain)
    if not last:
        whole_state = jnp.where(
            take,
            whole_state + whole_gain[:, None] * got_state,
            got_state + got_gain[:, None] * whole_state,
        )
        whole_gain = whole_gain * got_gain
    return (part_gain, part_state, whole_gain, whole_state)


def dp_sum(terms, axis):
    count = lax.axis_size(axis)
    if count != 4:
        return lax.psum(terms, axis)
    got = [lax.ppermute(terms, axis, [(i, i ^ k) for i in range(count)]) for k in (1, 2, 3)]
    return (terms + got[0]) + (got[1] + got[2])


def passed_along(block, axis, distance):
    devices = range(lax.axis_size(axis))
    route = [(i - distance, i) for i in devices if i - distance in devices]
    return lax.ppermute(block, axis, route)


def shift_pixels(values, shift_down, shift_right, row_width):
    pixel_count = values.shape[-1]
    offset = shift_down * row_width + shift_right
    padded = jnp.pad(values, [(0, 0)] * (values.ndim - 1) + [(row_width + 1, row_width + 1)])
    shifted = lax.slice_in_dim(
        padded, row_width + 1 + offset, row_width + 1 + offset + pixel_count, axis=values.ndim - 1
    )
    column = jnp.arange(pixel_count) % row_width + shift_right
    inside = (column >= 0) & (column < row_width)
    return jnp.where(inside, shifted, jnp.zeros_like(shifted))


def unfold(values, row_width):
    return jnp.concatenate([shift_pixels(values, a, b, row_width) for a, b in TAP_OFFSETS], axis=1)


def fold_taps(tap_grads, row_width):
    channels = tap_grads.shape[1] // 9
    accumulated = jnp.zeros((tap_grads.shape[0], channels, tap_grads.shape[2]), jnp.float32)
    for tap_index, (a, b) in enumerate(TAP_OFFSETS):
        piece = tap_grads[:, tap_index * channels : (tap_index + 1) * channels]
        accumulated = accumulated + shift_pixels(piece, -a, -b, row_width)
    return accumulated


def run_block(current, block_weights, step_size):
    inputs_kept = []
    for layer in range(block_weights.shape[0]):
        inputs_kept.append(current)
        squashed = jnp.tanh(current)
        patches = unfold(squashed.astype(jnp.bfloat16), WID)
        mixed = jnp.einsum(
            "ok,bkp->bop", block_weights[layer], patches, preferred_element_type=jnp.float32
        )
        current = current + step_size * mixed
    return (current, inputs_kept)


def back_block(inputs_kept, block_weights, upstream, step_size):
    layer_count = block_weights.shape[0]
    layer_grads = [None] * layer_count
    for layer in reversed(range(layer_count)):
        squashed = jnp.tanh(inputs_kept[layer])
        patches = unfold(squashed.astype(jnp.bfloat16), WID)
        scaled = (step_size * upstream).astype(jnp.bfloat16)
        layer_grads[layer] = jnp.einsum(
            "bop,bkp->ok", scaled, patches, preferred_element_type=jnp.float32
        )
        spread = jnp.einsum(
            "ok,bop->bkp", block_weights[layer], scaled, preferred_element_type=jnp.float32
        )
        upstream = upstream + (1.0 - squashed * squashed) * fold_taps(spread, WID)
    return (upstream, jnp.stack(layer_grads))


def body(cpoints, weights, coarse_gain, cotangent):
    step_size = 1.0 / (weights.shape[0] * lax.axis_size("depth"))
    rounds = (lax.axis_size("depth") - 1).bit_length()
    place = lax.axis_index("depth")
    own_state = cpoints[0]
    rate_vec = coarse_gain[0]
    cot_here = cotangent[0]
    leading = place == 0

    def before(bit):
        return (place >> bit) % 2 == 1

    def after(bit):
        return (place >> bit) % 2 == 0

    relaxed, own_kept = run_block(own_state, weights, step_size)
    arriving = passed_along(relaxed, "depth", 1)
    start_state = jnp.where(leading, own_state, arriving)
    propagated, start_kept = run_block(start_state, weights, step_size)
    gained_start = rate_vec[None, :, None] * start_state
    offset = propagated - jnp.where(leading, jnp.zeros_like(gained_start), gained_start)
    forward = (rate_vec, offset, rate_vec, offset)
    reverse = (jnp.ones_like(rate_vec), jnp.zeros_like(cot_here), rate_vec, rate_vec[None, :, None] * cot_here)
    for bit in range(rounds):
        got_f, got_r = exchange(
            (forward[2], reverse[2]), jnp.stack([forward[3], reverse[3]]), "depth", bit
        )
        forward = scan_round(forward, got_f, before, bit, bit == rounds - 1)
        reverse = scan_round(reverse, got_r, after, bit, bit == rounds - 1)
    passed_in = reverse[1]
    adjoint_here = cot_here + passed_in
    back_start, start_grads = back_block(start_kept, weights, adjoint_here, step_size)
    arriving_bar = passed_along(back_start, "depth", -1)
    relaxed_bar = arriving_bar - passed_in
    back_own, own_grads = back_block(own_kept, weights, relaxed_bar, step_size)
    corrected = forward[1]
    grad_cpoints = jnp.where(leading, back_own + back_start, back_own)
    grad_weights = dp_sum(start_grads + own_grads, "dp")
    return (corrected[None], grad_cpoints[None], grad_weights)


def solution(mesh):
    placed = (
        P("depth", "dp", None, None),
        P("depth", None, None),
        P("depth", None),
        P("depth", "dp", None, None),
    )
    return jax.shard_map(
        body,
        mesh=mesh,
        in_specs=placed,
        out_specs=(
            P("depth", "dp", None, None),
            P("depth", "dp", None, None),
            P("depth", None, None),
        ),
        check_vma=False,
    )
```

```python
import jax
import jax.numpy as jnp
from jax import lax
from jax.sharding import PartitionSpec as P

WID = 16


TAP_OFFSETS = [(-1, -1), (-1, 0), (-1, 1), (0, -1), (0, 0), (0, 1), (1, -1), (1, 0), (1, 1)]


def pack(gains, states):
    width = states.shape[-1]
    rows = [jnp.pad(g, (0, width - g.shape[0]))[None] for g in gains]
    return jnp.concatenate([states.reshape(-1, width)] + rows, axis=0)


def exchange(gains, states, axis, bit):
    count = lax.axis_size(axis)
    arrived = lax.ppermute(pack(gains, states), axis, [(i, i ^ (1 << bit)) for i in range(count)])
    rows = states.size // states.shape[-1]
    each = states.shape[1:]
    got = arrived[:rows].reshape(states.shape)
    return tuple(
        (arrived[rows + k, : g.shape[0]], got[k].reshape(each)) for k, g in enumerate(gains)
    )


def scan_round(scan, arrived, partner_first, bit, last):
    part_gain, part_state, whole_gain, whole_state = scan
    got_gain, got_state = arrived
    take = partner_first(bit)
    part_state = jnp.where(take, part_state + part_gain[:, None] * got_state, part_state)
    part_gain = jnp.where(take, part_gain * got_gain, part_gain)
    if not last:
        whole_state = jnp.where(
            take,
            whole_state + whole_gain[:, None] * got_state,
            got_state + got_gain[:, None] * whole_state,
        )
        whole_gain = whole_gain * got_gain
    return (part_gain, part_state, whole_gain, whole_state)


def dp_sum(terms, axis):
    count = lax.axis_size(axis)
    if count != terms.shape[0] or count & (count - 1):
        return lax.psum(terms, axis)
    place = lax.axis_index(axis)
    pairs = lambda k: [(i, i ^ k) for i in range(count)]
    got = [terms[place]] + [
        lax.ppermute(lax.dynamic_index_in_dim(terms, place ^ k, 0, False), axis, pairs(k))
        for k in range(1, count)
    ]
    total = got[0]
    for piece in got[1:]:
        total = total + piece
    back = jnp.stack([total] + [lax.ppermute(total, axis, pairs(k)) for k in range(1, count)])
    return jnp.take(back, jnp.arange(count) ^ place, axis=0)


def passed_along(block, axis, distance):
    devices = range(lax.axis_size(axis))
    route = [(i - distance, i) for i in devices if i - distance in devices]
    return lax.ppermute(block, axis, route)


def shift_pixels(values, shift_down, shift_right, row_width):
    pixel_count = values.shape[-1]
    offset = shift_down * row_width + shift_right
    padded = jnp.pad(values, [(0, 0)] * (values.ndim - 1) + [(row_width + 1, row_width + 1)])
    shifted = lax.slice_in_dim(
        padded, row_width + 1 + offset, row_width + 1 + offset + pixel_count, axis=values.ndim - 1
    )
    column = jnp.arange(pixel_count) % row_width + shift_right
    inside = (column >= 0) & (column < row_width)
    return jnp.where(inside, shifted, jnp.zeros_like(shifted))


def unfold(values, row_width):
    return jnp.concatenate([shift_pixels(values, a, b, row_width) for a, b in TAP_OFFSETS], axis=1)


def fold_taps(tap_grads, row_width):
    channels = tap_grads.shape[1] // 9
    accumulated = jnp.zeros((tap_grads.shape[0], channels, tap_grads.shape[2]), jnp.float32)
    for tap_index, (a, b) in enumerate(TAP_OFFSETS):
        piece = tap_grads[:, tap_index * channels : (tap_index + 1) * channels]
        accumulated = accumulated + shift_pixels(piece, -a, -b, row_width)
    return accumulated


def run_block(current, block_weights, step_size):
    inputs_kept = []
    for layer in range(block_weights.shape[0]):
        inputs_kept.append(current)
        squashed = jnp.tanh(current)
        patches = unfold(squashed.astype(jnp.bfloat16), WID)
        mixed = jnp.einsum(
            "ok,bkp->bop", block_weights[layer], patches, preferred_element_type=jnp.float32
        )
        current = current + step_size * mixed
    return (current, inputs_kept)


def back_block(inputs_kept, block_weights, upstream, step_size):
    layer_count = block_weights.shape[0]
    layer_grads = [None] * layer_count
    for layer in reversed(range(layer_count)):
        squashed = jnp.tanh(inputs_kept[layer])
        patches = unfold(squashed.astype(jnp.bfloat16), WID)
        scaled = (step_size * upstream).astype(jnp.bfloat16)
        layer_grads[layer] = jnp.einsum(
            "bop,bkp->ok", scaled, patches, preferred_element_type=jnp.float32
        )
        spread = jnp.einsum(
            "ok,bop->bkp", block_weights[layer], scaled, preferred_element_type=jnp.float32
        )
        upstream = upstream + (1.0 - squashed * squashed) * fold_taps(spread, WID)
    return (upstream, jnp.stack(layer_grads))


def body(cpoints, weights, coarse_gain, cotangent):
    step_size = 1.0 / (weights.shape[0] * lax.axis_size("depth"))
    rounds = (lax.axis_size("depth") - 1).bit_length()
    place = lax.axis_index("depth")
    own_state = cpoints[0]
    rate_vec = coarse_gain[0]
    cot_here = cotangent[0]
    leading = place == 0

    def before(bit):
        return (place >> bit) % 2 == 1

    def after(bit):
        return (place >> bit) % 2 == 0

    relaxed, own_kept = run_block(own_state, weights, step_size)
    arriving = passed_along(relaxed, "depth", 1)
    start_state = jnp.where(leading, own_state, arriving)
    propagated, start_kept = run_block(start_state, weights, step_size)
    gained_start = rate_vec[None, :, None] * start_state
    offset = propagated - jnp.where(leading, jnp.zeros_like(gained_start), gained_start)
    forward = (rate_vec, offset, rate_vec, offset)
    reverse = (jnp.ones_like(rate_vec), jnp.zeros_like(cot_here), rate_vec, rate_vec[None, :, None] * cot_here)
    for bit in range(rounds):
        got_f, got_r = exchange(
            (forward[2], reverse[2]), jnp.stack([forward[3], reverse[3]]), "depth", bit
        )
        forward = scan_round(forward, got_f, before, bit, bit == rounds - 1)
        reverse = scan_round(reverse, got_r, after, bit, bit == rounds - 1)
    passed_in = reverse[1]
    adjoint_here = cot_here + passed_in
    back_start, start_grads = back_block(start_kept, weights, adjoint_here, step_size)
    arriving_bar = passed_along(back_start, "depth", -1)
    relaxed_bar = arriving_bar - passed_in
    back_own, own_grads = back_block(own_kept, weights, relaxed_bar, step_size)
    corrected = forward[1]
    grad_cpoints = jnp.where(leading, back_own + back_start, back_own)
    grad_weights = dp_sum(start_grads + own_grads, "dp")
    return (corrected[None], grad_cpoints[None], grad_weights)


def solution(mesh):
    placed = (
        P("depth", "dp", None, None),
        P("depth", None, None),
        P("depth", None),
        P("depth", "dp", None, None),
    )
    return jax.shard_map(
        body,
        mesh=mesh,
        in_specs=placed,
        out_specs=(
            P("depth", "dp", None, None),
            P("depth", "dp", None, None),
            P("depth", None, None),
        ),
        check_vma=False,
    )
```

```python
import jax
import jax.numpy as jnp
from jax import lax
from jax.sharding import PartitionSpec as P

WID = 16


TAP_OFFSETS = [(-1, -1), (-1, 0), (-1, 1), (0, -1), (0, 0), (0, 1), (1, -1), (1, 0), (1, 1)]


def pack(gains, states):
    width = states.shape[-1]
    rows = [jnp.pad(g, (0, width - g.shape[0]))[None] for g in gains]
    return jnp.concatenate([states.reshape(-1, width)] + rows, axis=0)


def exchange(gains, states, axis, bit, mask=None):
    count = lax.axis_size(axis)
    mask = 1 << bit if mask is None else mask
    arrived = lax.ppermute(pack(gains, states), axis, [(i, i ^ mask) for i in range(count)])
    rows = states.size // states.shape[-1]
    each = states.shape[1:]
    got = arrived[:rows].reshape(states.shape)
    return tuple(
        (arrived[rows + k, : g.shape[0]], got[k].reshape(each)) for k, g in enumerate(gains)
    )


def last_two_rounds(forward, reverse, axis, bit, place):
    quarter = (place >> bit) % 4
    gains = (forward[2], reverse[2])
    states = jnp.stack([forward[3], reverse[3]])
    arrived = [exchange(gains, states, axis, bit, m << bit) for m in range(1, 4)]
    order = jnp.arange(4) ^ quarter
    results = []
    for k, (scan, earlier) in enumerate(((forward, True), (reverse, False))):
        slot_gain = jnp.take(jnp.stack([gains[k]] + [a[k][0] for a in arrived]), order, axis=0)
        slot_state = jnp.take(jnp.stack([states[k]] + [a[k][1] for a in arrived]), order, axis=0)
        steps = range(4) if earlier else reversed(range(4))
        running = jnp.zeros_like(slot_state[0])
        inner = [None] * 4
        for q in steps:
            inner[q] = running
            running = slot_state[q] + slot_gain[q][:, None] * running
        picked = lax.dynamic_index_in_dim(jnp.stack(inner), quarter, 0, False)
        results.append(scan[1] + scan[0][:, None] * picked)
    return results


def scan_round(scan, arrived, partner_first, bit, last):
    part_gain, part_state, whole_gain, whole_state = scan
    got_gain, got_state = arrived
    take = partner_first(bit)
    part_state = jnp.where(take, part_state + part_gain[:, None] * got_state, part_state)
    part_gain = jnp.where(take, part_gain * got_gain, part_gain)
    if not last:
        whole_state = jnp.where(
            take,
            whole_state + whole_gain[:, None] * got_state,
            got_state + got_gain[:, None] * whole_state,
        )
        whole_gain = whole_gain * got_gain
    return (part_gain, part_state, whole_gain, whole_state)


def dp_sum(terms, axis):
    count = lax.axis_size(axis)
    if count != terms.shape[0] or count & (count - 1):
        return lax.psum(terms, axis)
    place = lax.axis_index(axis)
    pairs = lambda k: [(i, i ^ k) for i in range(count)]
    got = [terms[place]] + [
        lax.ppermute(lax.dynamic_index_in_dim(terms, place ^ k, 0, False), axis, pairs(k))
        for k in range(1, count)
    ]
    total = got[0]
    for piece in got[1:]:
        total = total + piece
    back = jnp.stack([total] + [lax.ppermute(total, axis, pairs(k)) for k in range(1, count)])
    return jnp.take(back, jnp.arange(count) ^ place, axis=0)


def passed_along(block, axis, distance):
    devices = range(lax.axis_size(axis))
    route = [(i - distance, i) for i in devices if i - distance in devices]
    return lax.ppermute(block, axis, route)


def shift_pixels(values, shift_down, shift_right, row_width):
    pixel_count = values.shape[-1]
    offset = shift_down * row_width + shift_right
    padded = jnp.pad(values, [(0, 0)] * (values.ndim - 1) + [(row_width + 1, row_width + 1)])
    shifted = lax.slice_in_dim(
        padded, row_width + 1 + offset, row_width + 1 + offset + pixel_count, axis=values.ndim - 1
    )
    column = jnp.arange(pixel_count) % row_width + shift_right
    inside = (column >= 0) & (column < row_width)
    return jnp.where(inside, shifted, jnp.zeros_like(shifted))


def unfold(values, row_width):
    return jnp.concatenate([shift_pixels(values, a, b, row_width) for a, b in TAP_OFFSETS], axis=1)


def fold_taps(tap_grads, row_width):
    channels = tap_grads.shape[1] // 9
    accumulated = jnp.zeros((tap_grads.shape[0], channels, tap_grads.shape[2]), jnp.float32)
    for tap_index, (a, b) in enumerate(TAP_OFFSETS):
        piece = tap_grads[:, tap_index * channels : (tap_index + 1) * channels]
        accumulated = accumulated + shift_pixels(piece, -a, -b, row_width)
    return accumulated


def run_block(current, block_weights, step_size):
    inputs_kept = []
    for layer in range(block_weights.shape[0]):
        inputs_kept.append(current)
        squashed = jnp.tanh(current)
        patches = unfold(squashed.astype(jnp.bfloat16), WID)
        mixed = jnp.einsum(
            "ok,bkp->bop", block_weights[layer], patches, preferred_element_type=jnp.float32
        )
        current = current + step_size * mixed
    return (current, inputs_kept)


def back_block(inputs_kept, block_weights, upstream, step_size):
    layer_count = block_weights.shape[0]
    layer_grads = [None] * layer_count
    for layer in reversed(range(layer_count)):
        squashed = jnp.tanh(inputs_kept[layer])
        patches = unfold(squashed.astype(jnp.bfloat16), WID)
        scaled = (step_size * upstream).astype(jnp.bfloat16)
        layer_grads[layer] = jnp.einsum(
            "bop,bkp->ok", scaled, patches, preferred_element_type=jnp.float32
        )
        spread = jnp.einsum(
            "ok,bop->bkp", block_weights[layer], scaled, preferred_element_type=jnp.float32
        )
        upstream = upstream + (1.0 - squashed * squashed) * fold_taps(spread, WID)
    return (upstream, jnp.stack(layer_grads))


def body(cpoints, weights, coarse_gain, cotangent):
    step_size = 1.0 / (weights.shape[0] * lax.axis_size("depth"))
    rounds = (lax.axis_size("depth") - 1).bit_length()
    place = lax.axis_index("depth")
    own_state = cpoints[0]
    rate_vec = coarse_gain[0]
    cot_here = cotangent[0]
    leading = place == 0

    def before(bit):
        return (place >> bit) % 2 == 1

    def after(bit):
        return (place >> bit) % 2 == 0

    relaxed, own_kept = run_block(own_state, weights, step_size)
    arriving = passed_along(relaxed, "depth", 1)
    start_state = jnp.where(leading, own_state, arriving)
    propagated, start_kept = run_block(start_state, weights, step_size)
    gained_start = rate_vec[None, :, None] * start_state
    offset = propagated - jnp.where(leading, jnp.zeros_like(gained_start), gained_start)
    forward = (rate_vec, offset, rate_vec, offset)
    reverse = (jnp.ones_like(rate_vec), jnp.zeros_like(cot_here), rate_vec, rate_vec[None, :, None] * cot_here)
    binary = rounds - 2 if rounds >= 2 and lax.axis_size("depth") == 1 << rounds else rounds
    for bit in range(binary):
        got_f, got_r = exchange(
            (forward[2], reverse[2]), jnp.stack([forward[3], reverse[3]]), "depth", bit
        )
        forward = scan_round(forward, got_f, before, bit, bit == rounds - 1)
        reverse = scan_round(reverse, got_r, after, bit, bit == rounds - 1)
    if binary < rounds:
        corrected, passed_in = last_two_rounds(forward, reverse, "depth", binary, place)
    else:
        corrected, passed_in = forward[1], reverse[1]
    adjoint_here = cot_here + passed_in
    back_start, start_grads = back_block(start_kept, weights, adjoint_here, step_size)
    arriving_bar = passed_along(back_start, "depth", -1)
    relaxed_bar = arriving_bar - passed_in
    back_own, own_grads = back_block(own_kept, weights, relaxed_bar, step_size)
    grad_cpoints = jnp.where(leading, back_own + back_start, back_own)
    grad_weights = dp_sum(start_grads + own_grads, "dp")
    return (corrected[None], grad_cpoints[None], grad_weights)


def solution(mesh):
    placed = (
        P("depth", "dp", None, None),
        P("depth", None, None),
        P("depth", None),
        P("depth", "dp", None, None),
    )
    return jax.shard_map(
        body,
        mesh=mesh,
        in_specs=placed,
        out_specs=(
            P("depth", "dp", None, None),
            P("depth", "dp", None, None),
            P("depth", None, None),
        ),
        check_vma=False,
    )
```

```python
import jax
import jax.numpy as jnp
from jax import lax
from jax.sharding import PartitionSpec as P

WID = 16


TAP_OFFSETS = [(-1, -1), (-1, 0), (-1, 1), (0, -1), (0, 0), (0, 1), (1, -1), (1, 0), (1, 1)]


def pack(gains, states):
    width = states.shape[-1]
    rows = [jnp.pad(g, (0, width - g.shape[0]))[None] for g in gains]
    return jnp.concatenate([states.reshape(-1, width)] + rows, axis=0)


def exchange(gains, states, axis, bit):
    count = lax.axis_size(axis)
    arrived = lax.ppermute(pack(gains, states), axis, [(i, i ^ (1 << bit)) for i in range(count)])
    rows = states.size // states.shape[-1]
    each = states.shape[1:]
    got = arrived[:rows].reshape(states.shape)
    return tuple(
        (arrived[rows + k, : g.shape[0]], got[k].reshape(each)) for k, g in enumerate(gains)
    )


def scan_round(scan, arrived, partner_first, bit, last):
    part_gain, part_state, whole_gain, whole_state = scan
    got_gain, got_state = arrived
    take = partner_first(bit)
    part_state = jnp.where(take, part_state + part_gain[:, None] * got_state, part_state)
    part_gain = jnp.where(take, part_gain * got_gain, part_gain)
    if not last:
        whole_state = jnp.where(
            take,
            whole_state + whole_gain[:, None] * got_state,
            got_state + got_gain[:, None] * whole_state,
        )
        whole_gain = whole_gain * got_gain
    return (part_gain, part_state, whole_gain, whole_state)


def dp_sum(terms, axis):
    count = lax.axis_size(axis)
    if count != terms.shape[0] or count & (count - 1):
        return lax.psum(terms, axis)
    place = lax.axis_index(axis)
    pairs = lambda k: [(i, i ^ k) for i in range(count)]
    got = [terms[place]] + [
        lax.ppermute(lax.dynamic_index_in_dim(terms, place ^ k, 0, False), axis, pairs(k))
        for k in range(1, count)
    ]
    total = got[0]
    for piece in got[1:]:
        total = total + piece
    back = jnp.stack([total] + [lax.ppermute(total, axis, pairs(k)) for k in range(1, count)])
    return jnp.take(back, jnp.arange(count) ^ place, axis=0)


def passed_along(block, axis, distance):
    devices = range(lax.axis_size(axis))
    route = [(i - distance, i) for i in devices if i - distance in devices]
    return lax.ppermute(block, axis, route)


def shift_pixels(values, shift_down, shift_right, row_width):
    pixel_count = values.shape[-1]
    offset = shift_down * row_width + shift_right
    padded = jnp.pad(values, [(0, 0)] * (values.ndim - 1) + [(row_width + 1, row_width + 1)])
    shifted = lax.slice_in_dim(
        padded, row_width + 1 + offset, row_width + 1 + offset + pixel_count, axis=values.ndim - 1
    )
    column = jnp.arange(pixel_count) % row_width + shift_right
    inside = (column >= 0) & (column < row_width)
    return jnp.where(inside, shifted, jnp.zeros_like(shifted))


def unfold(values, row_width):
    return jnp.concatenate([shift_pixels(values, a, b, row_width) for a, b in TAP_OFFSETS], axis=1)


def fold_taps(tap_grads, row_width):
    channels = tap_grads.shape[1] // 9
    accumulated = jnp.zeros((tap_grads.shape[0], channels, tap_grads.shape[2]), jnp.float32)
    for tap_index, (a, b) in enumerate(TAP_OFFSETS):
        piece = tap_grads[:, tap_index * channels : (tap_index + 1) * channels]
        accumulated = accumulated + shift_pixels(piece, -a, -b, row_width)
    return accumulated


def run_block(current, block_weights, step_size):
    inputs_kept = []
    for layer in range(block_weights.shape[0]):
        inputs_kept.append(current)
        squashed = jnp.tanh(current)
        patches = unfold(squashed.astype(jnp.bfloat16), WID)
        mixed = jnp.einsum(
            "ok,bkp->bop", block_weights[layer], patches, preferred_element_type=jnp.float32
        )
        current = current + step_size * mixed
    return (current, inputs_kept)


def back_block(inputs_kept, block_weights, upstream, step_size):
    layer_count = block_weights.shape[0]
    layer_grads = [None] * layer_count
    for layer in reversed(range(layer_count)):
        squashed = jnp.tanh(inputs_kept[layer])
        patches = unfold(squashed.astype(jnp.bfloat16), WID)
        scaled = (step_size * upstream).astype(jnp.bfloat16)
        layer_grads[layer] = jnp.einsum(
            "bop,bkp->ok", scaled, patches, preferred_element_type=jnp.float32
        )
        spread = jnp.einsum(
            "ok,bop->bkp", block_weights[layer], scaled, preferred_element_type=jnp.float32
        )
        upstream = upstream + (1.0 - squashed * squashed) * fold_taps(spread, WID)
    return (upstream, jnp.stack(layer_grads))


def body(cpoints, weights, coarse_gain, cotangent):
    step_size = 1.0 / (weights.shape[0] * lax.axis_size("depth"))
    rounds = (lax.axis_size("depth") - 1).bit_length()
    place = lax.axis_index("depth")
    own_state = cpoints[0]
    rate_vec = coarse_gain[0]
    cot_here = cotangent[0]
    leading = place == 0

    def before(bit):
        return (place >> bit) % 2 == 1

    def after(bit):
        return (place >> bit) % 2 == 0

    relaxed, own_kept = run_block(own_state, weights, step_size)
    arriving = passed_along(relaxed, "depth", 1)
    start_state = jnp.where(leading, own_state, arriving)
    propagated, start_kept = run_block(start_state, weights, step_size)
    gained_start = rate_vec[None, :, None] * start_state
    offset = propagated - jnp.where(leading, jnp.zeros_like(gained_start), gained_start)
    forward = (rate_vec, offset, rate_vec, offset)
    reverse = (jnp.ones_like(rate_vec), jnp.zeros_like(cot_here), rate_vec, rate_vec[None, :, None] * cot_here)
    for bit in range(rounds):
        got_f, got_r = exchange(
            (forward[2], reverse[2]), jnp.stack([forward[3], reverse[3]]), "depth", bit
        )
        forward = scan_round(forward, got_f, before, bit, bit == rounds - 1)
        reverse = scan_round(reverse, got_r, after, bit, bit == rounds - 1)
    passed_in = reverse[1]
    adjoint_here = cot_here + passed_in
    back_start, start_grads = back_block(start_kept, weights, adjoint_here, step_size)
    arriving_bar = passed_along(back_start, "depth", -1)
    relaxed_bar = arriving_bar - passed_in
    back_own, own_grads = back_block(own_kept, weights, relaxed_bar, step_size)
    corrected = forward[1]
    grad_cpoints = jnp.where(leading, back_own + back_start, back_own)
    grad_weights = lax.all_gather(
        lax.psum_scatter(start_grads + own_grads, "dp", scatter_dimension=0, tiled=True),
        "dp",
        tiled=True,
    )
    return (corrected[None], grad_cpoints[None], grad_weights)


def solution(mesh):
    placed = (
        P("depth", "dp", None, None),
        P("depth", None, None),
        P("depth", None),
        P("depth", "dp", None, None),
    )
    return jax.shard_map(
        body,
        mesh=mesh,
        in_specs=placed,
        out_specs=(
            P("depth", "dp", None, None),
            P("depth", "dp", None, None),
            P("depth", None, None),
        ),
        check_vma=False,
    )
```

```python
import jax
import jax.numpy as jnp
from jax import lax
from jax.sharding import PartitionSpec as P
from jax.experimental import pallas as pl
from jax.experimental.pallas import tpu as pltpu

WID = 16


TAP_OFFSETS = [(-1, -1), (-1, 0), (-1, 1), (0, -1), (0, 0), (0, 1), (1, -1), (1, 0), (1, 1)]


def pack(gains, states):
    width = states.shape[-1]
    rows = [jnp.pad(g, (0, width - g.shape[0]))[None] for g in gains]
    return jnp.concatenate([states.reshape(-1, width)] + rows, axis=0)


def exchange(gains, states, axis, bit):
    count = lax.axis_size(axis)
    arrived = lax.ppermute(pack(gains, states), axis, [(i, i ^ (1 << bit)) for i in range(count)])
    rows = states.size // states.shape[-1]
    each = states.shape[1:]
    got = arrived[:rows].reshape(states.shape)
    return tuple(
        (arrived[rows + k, : g.shape[0]], got[k].reshape(each)) for k, g in enumerate(gains)
    )


def scan_round(scan, arrived, partner_first, bit, last):
    part_gain, part_state, whole_gain, whole_state = scan
    got_gain, got_state = arrived
    take = partner_first(bit)
    part_state = jnp.where(take, part_state + part_gain[:, None] * got_state, part_state)
    part_gain = jnp.where(take, part_gain * got_gain, part_gain)
    if not last:
        whole_state = jnp.where(
            take,
            whole_state + whole_gain[:, None] * got_state,
            got_state + got_gain[:, None] * whole_state,
        )
        whole_gain = whole_gain * got_gain
    return (part_gain, part_state, whole_gain, whole_state)


def round_kernel(take_ref, got_ref, part_ref, whole_ref, part_out, whole_out):
    channels = (got_ref.shape[0] - 2) // 2
    width = got_ref.shape[1]
    first = take_ref[0] == 1
    rows = lax.broadcasted_iota(jnp.int32, (channels, width), 0)
    lanes = lax.broadcasted_iota(jnp.int32, (channels, width), 1)

    def column(row):
        return jnp.sum(jnp.where(rows == lanes, jnp.broadcast_to(row, (channels, width)), 0.0), axis=1, keepdims=True)

    for k, take in enumerate((first, jnp.logical_not(first))):
        band = pl.ds(k * channels, channels)
        grow = pl.ds(2 * channels + k, 1)
        got_state, got_row = got_ref[band, :], got_ref[grow, :]
        part_state, part_row = part_ref[band, :], part_ref[grow, :]
        whole_state, whole_row = whole_ref[band, :], whole_ref[grow, :]
        part_out[band, :] = jnp.where(take, part_state + column(part_row) * got_state, part_state)
        part_out[grow, :] = jnp.where(take, part_row * got_row, part_row)
        whole_out[band, :] = jnp.where(
            take,
            whole_state + column(whole_row) * got_state,
            got_state + column(got_row) * whole_state,
        )
        whole_out[grow, :] = whole_row * got_row


def packed_round(take, got, part, whole):
    spec = pl.BlockSpec(memory_space=pltpu.VMEM)
    return pl.pallas_call(
        round_kernel,
        out_shape=(jax.ShapeDtypeStruct(part.shape, part.dtype),) * 2,
        in_specs=[pl.BlockSpec(memory_space=pltpu.SMEM), spec, spec, spec],
        out_specs=(spec, spec),
        cost_estimate=pl.CostEstimate(flops=12 * part.size, transcendentals=0, bytes_accessed=20 * part.size),
    )(take.astype(jnp.int32).reshape(1), got, part, whole)


def dp_sum(terms, axis):
    count = lax.axis_size(axis)
    if count != terms.shape[0] or count & (count - 1):
        return lax.psum(terms, axis)
    place = lax.axis_index(axis)
    pairs = lambda k: [(i, i ^ k) for i in range(count)]
    got = [terms[place]] + [
        lax.ppermute(lax.dynamic_index_in_dim(terms, place ^ k, 0, False), axis, pairs(k))
        for k in range(1, count)
    ]
    total = got[0]
    for piece in got[1:]:
        total = total + piece
    back = jnp.stack([total] + [lax.ppermute(total, axis, pairs(k)) for k in range(1, count)])
    return jnp.take(back, jnp.arange(count) ^ place, axis=0)


def passed_along(block, axis, distance):
    devices = range(lax.axis_size(axis))
    route = [(i - distance, i) for i in devices if i - distance in devices]
    return lax.ppermute(block, axis, route)


def shift_pixels(values, shift_down, shift_right, row_width):
    pixel_count = values.shape[-1]
    offset = shift_down * row_width + shift_right
    padded = jnp.pad(values, [(0, 0)] * (values.ndim - 1) + [(row_width + 1, row_width + 1)])
    shifted = lax.slice_in_dim(
        padded, row_width + 1 + offset, row_width + 1 + offset + pixel_count, axis=values.ndim - 1
    )
    column = jnp.arange(pixel_count) % row_width + shift_right
    inside = (column >= 0) & (column < row_width)
    return jnp.where(inside, shifted, jnp.zeros_like(shifted))


def unfold(values, row_width):
    return jnp.concatenate([shift_pixels(values, a, b, row_width) for a, b in TAP_OFFSETS], axis=1)


def fold_taps(tap_grads, row_width):
    channels = tap_grads.shape[1] // 9
    accumulated = jnp.zeros((tap_grads.shape[0], channels, tap_grads.shape[2]), jnp.float32)
    for tap_index, (a, b) in enumerate(TAP_OFFSETS):
        piece = tap_grads[:, tap_index * channels : (tap_index + 1) * channels]
        accumulated = accumulated + shift_pixels(piece, -a, -b, row_width)
    return accumulated


def run_block(current, block_weights, step_size):
    inputs_kept = []
    for layer in range(block_weights.shape[0]):
        inputs_kept.append(current)
        squashed = jnp.tanh(current)
        patches = unfold(squashed.astype(jnp.bfloat16), WID)
        mixed = jnp.einsum(
            "ok,bkp->bop", block_weights[layer], patches, preferred_element_type=jnp.float32
        )
        current = current + step_size * mixed
    return (current, inputs_kept)


def back_block(inputs_kept, block_weights, upstream, step_size):
    layer_count = block_weights.shape[0]
    layer_grads = [None] * layer_count
    for layer in reversed(range(layer_count)):
        squashed = jnp.tanh(inputs_kept[layer])
        patches = unfold(squashed.astype(jnp.bfloat16), WID)
        scaled = (step_size * upstream).astype(jnp.bfloat16)
        layer_grads[layer] = jnp.einsum(
            "bop,bkp->ok", scaled, patches, preferred_element_type=jnp.float32
        )
        spread = jnp.einsum(
            "ok,bop->bkp", block_weights[layer], scaled, preferred_element_type=jnp.float32
        )
        upstream = upstream + (1.0 - squashed * squashed) * fold_taps(spread, WID)
    return (upstream, jnp.stack(layer_grads))


def body(cpoints, weights, coarse_gain, cotangent):
    step_size = 1.0 / (weights.shape[0] * lax.axis_size("depth"))
    rounds = (lax.axis_size("depth") - 1).bit_length()
    place = lax.axis_index("depth")
    own_state = cpoints[0]
    rate_vec = coarse_gain[0]
    cot_here = cotangent[0]
    leading = place == 0

    def before(bit):
        return (place >> bit) % 2 == 1

    def after(bit):
        return (place >> bit) % 2 == 0

    relaxed, own_kept = run_block(own_state, weights, step_size)
    arriving = passed_along(relaxed, "depth", 1)
    start_state = jnp.where(leading, own_state, arriving)
    propagated, start_kept = run_block(start_state, weights, step_size)
    gained_start = rate_vec[None, :, None] * start_state
    offset = propagated - jnp.where(leading, jnp.zeros_like(gained_start), gained_start)
    channels = offset.shape[-2]
    pair = lambda a, b: jnp.stack([a, b]).reshape(2 * channels, -1)
    part = pack((rate_vec, jnp.ones_like(rate_vec)), pair(offset, jnp.zeros_like(cot_here)))
    whole = pack((rate_vec, rate_vec), pair(offset, rate_vec[None, :, None] * cot_here))
    for bit in range(rounds):
        got = lax.ppermute(whole, "depth", [(i, i ^ (1 << bit)) for i in range(lax.axis_size("depth"))])
        part, whole = packed_round(before(bit), got, part, whole)
    corrected = part[:channels].reshape(offset.shape)
    passed_in = part[channels : 2 * channels].reshape(cot_here.shape)
    adjoint_here = cot_here + passed_in
    back_start, start_grads = back_block(start_kept, weights, adjoint_here, step_size)
    arriving_bar = passed_along(back_start, "depth", -1)
    relaxed_bar = arriving_bar - passed_in
    back_own, own_grads = back_block(own_kept, weights, relaxed_bar, step_size)
    grad_cpoints = jnp.where(leading, back_own + back_start, back_own)
    grad_weights = dp_sum(start_grads + own_grads, "dp")
    return (corrected[None], grad_cpoints[None], grad_weights)


def solution(mesh):
    placed = (
        P("depth", "dp", None, None),
        P("depth", None, None),
        P("depth", None),
        P("depth", "dp", None, None),
    )
    return jax.shard_map(
        body,
        mesh=mesh,
        in_specs=placed,
        out_specs=(
            P("depth", "dp", None, None),
            P("depth", "dp", None, None),
            P("depth", None, None),
        ),
        check_vma=False,
    )
```

```python
import jax
import jax.numpy as jnp
from jax import lax
from jax.sharding import PartitionSpec as P
from jax.experimental import pallas as pl
from jax.experimental.pallas import tpu as pltpu

WID = 16


TAP_OFFSETS = [(-1, -1), (-1, 0), (-1, 1), (0, -1), (0, 0), (0, 1), (1, -1), (1, 0), (1, 1)]


def pack(gains, states):
    width = states.shape[-1]
    rows = [jnp.pad(g, (0, width - g.shape[0]))[None] for g in gains]
    return jnp.concatenate([states.reshape(-1, width)] + rows, axis=0)


def exchange(gains, states, axis, bit):
    count = lax.axis_size(axis)
    arrived = lax.ppermute(pack(gains, states), axis, [(i, i ^ (1 << bit)) for i in range(count)])
    rows = states.size // states.shape[-1]
    each = states.shape[1:]
    got = arrived[:rows].reshape(states.shape)
    return tuple(
        (arrived[rows + k, : g.shape[0]], got[k].reshape(each)) for k, g in enumerate(gains)
    )


def scan_round(scan, arrived, partner_first, bit, last):
    part_gain, part_state, whole_gain, whole_state = scan
    got_gain, got_state = arrived
    take = partner_first(bit)
    part_state = jnp.where(take, part_state + part_gain[:, None] * got_state, part_state)
    part_gain = jnp.where(take, part_gain * got_gain, part_gain)
    if not last:
        whole_state = jnp.where(
            take,
            whole_state + whole_gain[:, None] * got_state,
            got_state + got_gain[:, None] * whole_state,
        )
        whole_gain = whole_gain * got_gain
    return (part_gain, part_state, whole_gain, whole_state)


def round_kernel(take_ref, got_ref, part_ref, whole_ref, part_out, whole_out):
    channels = got_ref.shape[0] // 2
    width = got_ref.shape[1] - 128
    first = take_ref[0] == 1
    for k, take in enumerate((first, jnp.logical_not(first))):
        band = pl.ds(k * channels, channels)
        state, gain, col = pl.ds(0, width), pl.ds(width, 128), pl.ds(width, 1)
        got_state, got_gain = got_ref[band, state], got_ref[band, gain]
        part_state, part_gain = part_ref[band, state], part_ref[band, gain]
        whole_state, whole_gain = whole_ref[band, state], whole_ref[band, gain]
        part_out[band, state] = jnp.where(take, part_state + part_ref[band, col] * got_state, part_state)
        part_out[band, gain] = jnp.where(take, part_gain * got_gain, part_gain)
        whole_out[band, state] = jnp.where(
            take,
            whole_state + whole_ref[band, col] * got_state,
            got_state + got_ref[band, col] * whole_state,
        )
        whole_out[band, gain] = whole_gain * got_gain


def packed_round(take, got, part, whole):
    spec = pl.BlockSpec(memory_space=pltpu.VMEM)
    return pl.pallas_call(
        round_kernel,
        out_shape=(jax.ShapeDtypeStruct(part.shape, part.dtype),) * 2,
        in_specs=[pl.BlockSpec(memory_space=pltpu.SMEM), spec, spec, spec],
        out_specs=(spec, spec),
        cost_estimate=pl.CostEstimate(flops=12 * part.size, transcendentals=0, bytes_accessed=20 * part.size),
    )(take.astype(jnp.int32).reshape(1), got, part, whole)


def dp_sum(terms, axis):
    count = lax.axis_size(axis)
    if count != terms.shape[0] or count & (count - 1):
        return lax.psum(terms, axis)
    place = lax.axis_index(axis)
    pairs = lambda k: [(i, i ^ k) for i in range(count)]
    got = [terms[place]] + [
        lax.ppermute(lax.dynamic_index_in_dim(terms, place ^ k, 0, False), axis, pairs(k))
        for k in range(1, count)
    ]
    total = got[0]
    for piece in got[1:]:
        total = total + piece
    back = jnp.stack([total] + [lax.ppermute(total, axis, pairs(k)) for k in range(1, count)])
    return jnp.take(back, jnp.arange(count) ^ place, axis=0)


def passed_along(block, axis, distance):
    devices = range(lax.axis_size(axis))
    route = [(i - distance, i) for i in devices if i - distance in devices]
    return lax.ppermute(block, axis, route)


def shift_pixels(values, shift_down, shift_right, row_width):
    pixel_count = values.shape[-1]
    offset = shift_down * row_width + shift_right
    padded = jnp.pad(values, [(0, 0)] * (values.ndim - 1) + [(row_width + 1, row_width + 1)])
    shifted = lax.slice_in_dim(
        padded, row_width + 1 + offset, row_width + 1 + offset + pixel_count, axis=values.ndim - 1
    )
    column = jnp.arange(pixel_count) % row_width + shift_right
    inside = (column >= 0) & (column < row_width)
    return jnp.where(inside, shifted, jnp.zeros_like(shifted))


def unfold(values, row_width):
    return jnp.concatenate([shift_pixels(values, a, b, row_width) for a, b in TAP_OFFSETS], axis=1)


def fold_taps(tap_grads, row_width):
    channels = tap_grads.shape[1] // 9
    accumulated = jnp.zeros((tap_grads.shape[0], channels, tap_grads.shape[2]), jnp.float32)
    for tap_index, (a, b) in enumerate(TAP_OFFSETS):
        piece = tap_grads[:, tap_index * channels : (tap_index + 1) * channels]
        accumulated = accumulated + shift_pixels(piece, -a, -b, row_width)
    return accumulated


def run_block(current, block_weights, step_size):
    inputs_kept = []
    for layer in range(block_weights.shape[0]):
        inputs_kept.append(current)
        squashed = jnp.tanh(current)
        patches = unfold(squashed.astype(jnp.bfloat16), WID)
        mixed = jnp.einsum(
            "ok,bkp->bop", block_weights[layer], patches, preferred_element_type=jnp.float32
        )
        current = current + step_size * mixed
    return (current, inputs_kept)


def back_block(inputs_kept, block_weights, upstream, step_size):
    layer_count = block_weights.shape[0]
    layer_grads = [None] * layer_count
    for layer in reversed(range(layer_count)):
        squashed = jnp.tanh(inputs_kept[layer])
        patches = unfold(squashed.astype(jnp.bfloat16), WID)
        scaled = (step_size * upstream).astype(jnp.bfloat16)
        layer_grads[layer] = jnp.einsum(
            "bop,bkp->ok", scaled, patches, preferred_element_type=jnp.float32
        )
        spread = jnp.einsum(
            "ok,bop->bkp", block_weights[layer], scaled, preferred_element_type=jnp.float32
        )
        upstream = upstream + (1.0 - squashed * squashed) * fold_taps(spread, WID)
    return (upstream, jnp.stack(layer_grads))


def body(cpoints, weights, coarse_gain, cotangent):
    step_size = 1.0 / (weights.shape[0] * lax.axis_size("depth"))
    rounds = (lax.axis_size("depth") - 1).bit_length()
    place = lax.axis_index("depth")
    own_state = cpoints[0]
    rate_vec = coarse_gain[0]
    cot_here = cotangent[0]
    leading = place == 0

    def before(bit):
        return (place >> bit) % 2 == 1

    def after(bit):
        return (place >> bit) % 2 == 0

    relaxed, own_kept = run_block(own_state, weights, step_size)
    arriving = passed_along(relaxed, "depth", 1)
    start_state = jnp.where(leading, own_state, arriving)
    propagated, start_kept = run_block(start_state, weights, step_size)
    gained_start = rate_vec[None, :, None] * start_state
    offset = propagated - jnp.where(leading, jnp.zeros_like(gained_start), gained_start)
    channels = offset.shape[-2]
    def pair(gains, states):
        rows = [
            jnp.concatenate([s.reshape(channels, -1), jnp.broadcast_to(g[:, None], (channels, 128))], axis=1)
            for g, s in zip(gains, states)
        ]
        return jnp.concatenate(rows, axis=0)

    part = pair((rate_vec, jnp.ones_like(rate_vec)), (offset, jnp.zeros_like(cot_here)))
    whole = pair((rate_vec, rate_vec), (offset, rate_vec[None, :, None] * cot_here))
    for bit in range(rounds):
        got = lax.ppermute(whole, "depth", [(i, i ^ (1 << bit)) for i in range(lax.axis_size("depth"))])
        part, whole = packed_round(before(bit), got, part, whole)
    pixels = offset.shape[-1]
    corrected = part[:channels, :pixels].reshape(offset.shape)
    passed_in = part[channels : 2 * channels, :pixels].reshape(cot_here.shape)
    adjoint_here = cot_here + passed_in
    back_start, start_grads = back_block(start_kept, weights, adjoint_here, step_size)
    arriving_bar = passed_along(back_start, "depth", -1)
    relaxed_bar = arriving_bar - passed_in
    back_own, own_grads = back_block(own_kept, weights, relaxed_bar, step_size)
    grad_cpoints = jnp.where(leading, back_own + back_start, back_own)
    grad_weights = dp_sum(start_grads + own_grads, "dp")
    return (corrected[None], grad_cpoints[None], grad_weights)


def solution(mesh):
    placed = (
        P("depth", "dp", None, None),
        P("depth", None, None),
        P("depth", None),
        P("depth", "dp", None, None),
    )
    return jax.shard_map(
        body,
        mesh=mesh,
        in_specs=placed,
        out_specs=(
            P("depth", "dp", None, None),
            P("depth", "dp", None, None),
            P("depth", None, None),
        ),
        check_vma=False,
    )
```

```python
import jax
import jax.numpy as jnp
from jax import lax
from jax.sharding import PartitionSpec as P

WID = 16


TAP_OFFSETS = [(-1, -1), (-1, 0), (-1, 1), (0, -1), (0, 0), (0, 1), (1, -1), (1, 0), (1, 1)]


def pack(gains, states):
    width = states.shape[-1]
    rows = [jnp.pad(g, (0, width - g.shape[0]))[None] for g in gains]
    return jnp.concatenate([states.reshape(-1, width)] + rows, axis=0)


def exchange(gains, states, axis, bit):
    count = lax.axis_size(axis)
    arrived = lax.ppermute(pack(gains, states), axis, [(i, i ^ (1 << bit)) for i in range(count)])
    rows = states.size // states.shape[-1]
    each = states.shape[1:]
    got = arrived[:rows].reshape(states.shape)
    return tuple(
        (arrived[rows + k, : g.shape[0]], got[k].reshape(each)) for k, g in enumerate(gains)
    )


def scan_round(scan, arrived, partner_first, bit, last):
    part_gain, part_state, whole_gain, whole_state = scan
    got_gain, got_state = arrived
    take = partner_first(bit)
    part_state = jnp.where(take, part_state + part_gain[:, None] * got_state, part_state)
    part_gain = jnp.where(take, part_gain * got_gain, part_gain)
    if not last:
        whole_state = jnp.where(
            take,
            whole_state + whole_gain[:, None] * got_state,
            got_state + got_gain[:, None] * whole_state,
        )
        whole_gain = whole_gain * got_gain
    return (part_gain, part_state, whole_gain, whole_state)


def dp_sum(terms, axis):
    count = lax.axis_size(axis)
    if count & (count - 1):
        return lax.psum(terms, axis)
    step = 1
    while step < count:
        terms = terms + lax.ppermute(terms, axis, [(i, i ^ step) for i in range(count)])
        step *= 2
    return terms


def passed_along(block, axis, distance):
    devices = range(lax.axis_size(axis))
    route = [(i - distance, i) for i in devices if i - distance in devices]
    return lax.ppermute(block, axis, route)


def shift_pixels(values, shift_down, shift_right, row_width):
    pixel_count = values.shape[-1]
    offset = shift_down * row_width + shift_right
    padded = jnp.pad(values, [(0, 0)] * (values.ndim - 1) + [(row_width + 1, row_width + 1)])
    shifted = lax.slice_in_dim(
        padded, row_width + 1 + offset, row_width + 1 + offset + pixel_count, axis=values.ndim - 1
    )
    column = jnp.arange(pixel_count) % row_width + shift_right
    inside = (column >= 0) & (column < row_width)
    return jnp.where(inside, shifted, jnp.zeros_like(shifted))


def unfold(values, row_width):
    return jnp.concatenate([shift_pixels(values, a, b, row_width) for a, b in TAP_OFFSETS], axis=1)


def fold_taps(tap_grads, row_width):
    channels = tap_grads.shape[1] // 9
    accumulated = jnp.zeros((tap_grads.shape[0], channels, tap_grads.shape[2]), jnp.float32)
    for tap_index, (a, b) in enumerate(TAP_OFFSETS):
        piece = tap_grads[:, tap_index * channels : (tap_index + 1) * channels]
        accumulated = accumulated + shift_pixels(piece, -a, -b, row_width)
    return accumulated


def run_block(current, block_weights, step_size):
    inputs_kept = []
    for layer in range(block_weights.shape[0]):
        inputs_kept.append(current)
        squashed = jnp.tanh(current)
        patches = unfold(squashed.astype(jnp.bfloat16), WID)
        mixed = jnp.einsum(
            "ok,bkp->bop", block_weights[layer], patches, preferred_element_type=jnp.float32
        )
        current = current + step_size * mixed
    return (current, inputs_kept)


def back_block(inputs_kept, block_weights, upstream, step_size):
    layer_count = block_weights.shape[0]
    layer_grads = [None] * layer_count
    for layer in reversed(range(layer_count)):
        squashed = jnp.tanh(inputs_kept[layer])
        patches = unfold(squashed.astype(jnp.bfloat16), WID)
        scaled = (step_size * upstream).astype(jnp.bfloat16)
        layer_grads[layer] = jnp.einsum(
            "bop,bkp->ok", scaled, patches, preferred_element_type=jnp.float32
        )
        spread = jnp.einsum(
            "ok,bop->bkp", block_weights[layer], scaled, preferred_element_type=jnp.float32
        )
        upstream = upstream + (1.0 - squashed * squashed) * fold_taps(spread, WID)
    return (upstream, jnp.stack(layer_grads))


def body(cpoints, weights, coarse_gain, cotangent):
    step_size = 1.0 / (weights.shape[0] * lax.axis_size("depth"))
    rounds = (lax.axis_size("depth") - 1).bit_length()
    place = lax.axis_index("depth")
    own_state = cpoints[0]
    rate_vec = coarse_gain[0]
    cot_here = cotangent[0]
    leading = place == 0

    def before(bit):
        return (place >> bit) % 2 == 1

    def after(bit):
        return (place >> bit) % 2 == 0

    relaxed, own_kept = run_block(own_state, weights, step_size)
    arriving = passed_along(relaxed, "depth", 1)
    start_state = jnp.where(leading, own_state, arriving)
    propagated, start_kept = run_block(start_state, weights, step_size)
    gained_start = rate_vec[None, :, None] * start_state
    offset = propagated - jnp.where(leading, jnp.zeros_like(gained_start), gained_start)
    forward = (rate_vec, offset, rate_vec, offset)
    reverse = (jnp.ones_like(rate_vec), jnp.zeros_like(cot_here), rate_vec, rate_vec[None, :, None] * cot_here)
    for bit in range(rounds):
        got_f, got_r = exchange(
            (forward[2], reverse[2]), jnp.stack([forward[3], reverse[3]]), "depth", bit
        )
        forward = scan_round(forward, got_f, before, bit, bit == rounds - 1)
        reverse = scan_round(reverse, got_r, after, bit, bit == rounds - 1)
    passed_in = reverse[1]
    adjoint_here = cot_here + passed_in
    back_start, start_grads = back_block(start_kept, weights, adjoint_here, step_size)
    arriving_bar = passed_along(back_start, "depth", -1)
    relaxed_bar = arriving_bar - passed_in
    back_own, own_grads = back_block(own_kept, weights, relaxed_bar, step_size)
    corrected = forward[1]
    grad_cpoints = jnp.where(leading, back_own + back_start, back_own)
    grad_weights = dp_sum(start_grads + own_grads, "dp")
    return (corrected[None], grad_cpoints[None], grad_weights)


def solution(mesh):
    placed = (
        P("depth", "dp", None, None),
        P("depth", None, None),
        P("depth", None),
        P("depth", "dp", None, None),
    )
    return jax.shard_map(
        body,
        mesh=mesh,
        in_specs=placed,
        out_specs=(
            P("depth", "dp", None, None),
            P("depth", "dp", None, None),
            P("depth", None, None),
        ),
        check_vma=False,
    )
```

```python
import functools

import jax
import jax.numpy as jnp
from jax import lax
from jax.sharding import PartitionSpec as P
from jax.experimental import pallas as pl
from jax.experimental.pallas import tpu as pltpu

WID = 16


TAP_OFFSETS = [(-1, -1), (-1, 0), (-1, 1), (0, -1), (0, 0), (0, 1), (1, -1), (1, 0), (1, 1)]


def pack(gains, states):
    width = states.shape[-1]
    rows = [jnp.pad(g, (0, width - g.shape[0]))[None] for g in gains]
    return jnp.concatenate([states.reshape(-1, width)] + rows, axis=0)


def exchange(gains, states, axis, bit):
    count = lax.axis_size(axis)
    arrived = lax.ppermute(pack(gains, states), axis, [(i, i ^ (1 << bit)) for i in range(count)])
    rows = states.size // states.shape[-1]
    each = states.shape[1:]
    got = arrived[:rows].reshape(states.shape)
    return tuple(
        (arrived[rows + k, : g.shape[0]], got[k].reshape(each)) for k, g in enumerate(gains)
    )


def scan_round(scan, arrived, partner_first, bit, last):
    part_gain, part_state, whole_gain, whole_state = scan
    got_gain, got_state = arrived
    take = partner_first(bit)
    part_state = jnp.where(take, part_state + part_gain[:, None] * got_state, part_state)
    part_gain = jnp.where(take, part_gain * got_gain, part_gain)
    if not last:
        whole_state = jnp.where(
            take,
            whole_state + whole_gain[:, None] * got_state,
            got_state + got_gain[:, None] * whole_state,
        )
        whole_gain = whole_gain * got_gain
    return (part_gain, part_state, whole_gain, whole_state)


def dp_sum(terms, axis):
    count = lax.axis_size(axis)
    if count != terms.shape[0] or count & (count - 1):
        return lax.psum(terms, axis)
    place = lax.axis_index(axis)
    pairs = lambda k: [(i, i ^ k) for i in range(count)]
    got = [terms[place]] + [
        lax.ppermute(lax.dynamic_index_in_dim(terms, place ^ k, 0, False), axis, pairs(k))
        for k in range(1, count)
    ]
    total = got[0]
    for piece in got[1:]:
        total = total + piece
    back = jnp.stack([total] + [lax.ppermute(total, axis, pairs(k)) for k in range(1, count)])
    return jnp.take(back, jnp.arange(count) ^ place, axis=0)


def passed_along(block, axis, distance):
    devices = range(lax.axis_size(axis))
    route = [(i - distance, i) for i in devices if i - distance in devices]
    return lax.ppermute(block, axis, route)


def shift_pixels(values, shift_down, shift_right, row_width):
    pixel_count = values.shape[-1]
    offset = shift_down * row_width + shift_right
    padded = jnp.pad(values, [(0, 0)] * (values.ndim - 1) + [(row_width + 1, row_width + 1)])
    shifted = lax.slice_in_dim(
        padded, row_width + 1 + offset, row_width + 1 + offset + pixel_count, axis=values.ndim - 1
    )
    column = jnp.arange(pixel_count) % row_width + shift_right
    inside = (column >= 0) & (column < row_width)
    return jnp.where(inside, shifted, jnp.zeros_like(shifted))


def unfold(values, row_width):
    return jnp.concatenate([shift_pixels(values, a, b, row_width) for a, b in TAP_OFFSETS], axis=1)


def fold_taps(tap_grads, row_width):
    channels = tap_grads.shape[1] // 9
    accumulated = jnp.zeros((tap_grads.shape[0], channels, tap_grads.shape[2]), jnp.float32)
    for tap_index, (a, b) in enumerate(TAP_OFFSETS):
        piece = tap_grads[:, tap_index * channels : (tap_index + 1) * channels]
        accumulated = accumulated + shift_pixels(piece, -a, -b, row_width)
    return accumulated


def block_kernel(step_size, state_ref, weight_ref, out_ref, kept_ref):
    current = state_ref[...]
    pixels = current.shape[-1]
    place = lax.broadcasted_iota(jnp.int32, (1, pixels), 1)
    row, column = place // WID, place % WID
    for layer in range(weight_ref.shape[0]):
        kept_ref[layer] = current
        squashed = jnp.tanh(current)
        pieces = []
        for down, right in TAP_OFFSETS:
            shift = down * WID + right
            moved = pltpu.roll(squashed, (-shift) % pixels, 1) if shift else squashed
            inside = (row + down >= 0) & (row + down < WID) & (column + right >= 0) & (column + right < WID)
            pieces.append(jnp.where(inside, moved, 0.0).astype(jnp.bfloat16))
        patches = jnp.concatenate(pieces, axis=0)
        mixed = jnp.dot(weight_ref[layer], patches, preferred_element_type=jnp.float32)
        current = current + step_size * mixed
    out_ref[...] = current


def run_block(current, block_weights, step_size):
    layers, channels, pixels = block_weights.shape[0], current.shape[-2], current.shape[-1]
    spec = pl.BlockSpec(memory_space=pltpu.VMEM)
    out, kept = pl.pallas_call(
        functools.partial(block_kernel, step_size),
        out_shape=(
            jax.ShapeDtypeStruct((channels, pixels), jnp.float32),
            jax.ShapeDtypeStruct((layers, channels, pixels), jnp.float32),
        ),
        in_specs=[spec, spec],
        out_specs=(spec, spec),
        cost_estimate=pl.CostEstimate(
            flops=2 * layers * channels * block_weights.shape[-1] * pixels,
            transcendentals=layers * channels * pixels,
            bytes_accessed=4 * (layers + 2) * channels * pixels + 2 * block_weights.size,
        ),
    )(current.reshape(channels, pixels), block_weights)
    return (out.reshape(current.shape), [kept[k].reshape(current.shape) for k in range(layers)])


def back_block(inputs_kept, block_weights, upstream, step_size):
    layer_count = block_weights.shape[0]
    layer_grads = [None] * layer_count
    for layer in reversed(range(layer_count)):
        squashed = jnp.tanh(inputs_kept[layer])
        patches = unfold(squashed.astype(jnp.bfloat16), WID)
        scaled = (step_size * upstream).astype(jnp.bfloat16)
        layer_grads[layer] = jnp.einsum(
            "bop,bkp->ok", scaled, patches, preferred_element_type=jnp.float32
        )
        spread = jnp.einsum(
            "ok,bop->bkp", block_weights[layer], scaled, preferred_element_type=jnp.float32
        )
        upstream = upstream + (1.0 - squashed * squashed) * fold_taps(spread, WID)
    return (upstream, jnp.stack(layer_grads))


def body(cpoints, weights, coarse_gain, cotangent):
    step_size = 1.0 / (weights.shape[0] * lax.axis_size("depth"))
    rounds = (lax.axis_size("depth") - 1).bit_length()
    place = lax.axis_index("depth")
    own_state = cpoints[0]
    rate_vec = coarse_gain[0]
    cot_here = cotangent[0]
    leading = place == 0

    def before(bit):
        return (place >> bit) % 2 == 1

    def after(bit):
        return (place >> bit) % 2 == 0

    relaxed, own_kept = run_block(own_state, weights, step_size)
    arriving = passed_along(relaxed, "depth", 1)
    start_state = jnp.where(leading, own_state, arriving)
    propagated, start_kept = run_block(start_state, weights, step_size)
    gained_start = rate_vec[None, :, None] * start_state
    offset = propagated - jnp.where(leading, jnp.zeros_like(gained_start), gained_start)
    forward = (rate_vec, offset, rate_vec, offset)
    reverse = (jnp.ones_like(rate_vec), jnp.zeros_like(cot_here), rate_vec, rate_vec[None, :, None] * cot_here)
    for bit in range(rounds):
        got_f, got_r = exchange(
            (forward[2], reverse[2]), jnp.stack([forward[3], reverse[3]]), "depth", bit
        )
        forward = scan_round(forward, got_f, before, bit, bit == rounds - 1)
        reverse = scan_round(reverse, got_r, after, bit, bit == rounds - 1)
    passed_in = reverse[1]
    adjoint_here = cot_here + passed_in
    back_start, start_grads = back_block(start_kept, weights, adjoint_here, step_size)
    arriving_bar = passed_along(back_start, "depth", -1)
    relaxed_bar = arriving_bar - passed_in
    back_own, own_grads = back_block(own_kept, weights, relaxed_bar, step_size)
    corrected = forward[1]
    grad_cpoints = jnp.where(leading, back_own + back_start, back_own)
    grad_weights = dp_sum(start_grads + own_grads, "dp")
    return (corrected[None], grad_cpoints[None], grad_weights)


def solution(mesh):
    placed = (
        P("depth", "dp", None, None),
        P("depth", None, None),
        P("depth", None),
        P("depth", "dp", None, None),
    )
    return jax.shard_map(
        body,
        mesh=mesh,
        in_specs=placed,
        out_specs=(
            P("depth", "dp", None, None),
            P("depth", "dp", None, None),
            P("depth", None, None),
        ),
        check_vma=False,
    )
```

```python
import functools

import jax
import jax.numpy as jnp
from jax import lax
from jax.sharding import PartitionSpec as P
from jax.experimental import pallas as pl
from jax.experimental.pallas import tpu as pltpu

WID = 16


TAP_OFFSETS = [(-1, -1), (-1, 0), (-1, 1), (0, -1), (0, 0), (0, 1), (1, -1), (1, 0), (1, 1)]


def pack(gains, states):
    width = states.shape[-1]
    rows = [jnp.pad(g, (0, width - g.shape[0]))[None] for g in gains]
    return jnp.concatenate([states.reshape(-1, width)] + rows, axis=0)


def exchange(gains, states, axis, bit):
    count = lax.axis_size(axis)
    arrived = lax.ppermute(pack(gains, states), axis, [(i, i ^ (1 << bit)) for i in range(count)])
    rows = states.size // states.shape[-1]
    each = states.shape[1:]
    got = arrived[:rows].reshape(states.shape)
    return tuple(
        (arrived[rows + k, : g.shape[0]], got[k].reshape(each)) for k, g in enumerate(gains)
    )


def scan_round(scan, arrived, partner_first, bit, last):
    part_gain, part_state, whole_gain, whole_state = scan
    got_gain, got_state = arrived
    take = partner_first(bit)
    part_state = jnp.where(take, part_state + part_gain[:, None] * got_state, part_state)
    part_gain = jnp.where(take, part_gain * got_gain, part_gain)
    if not last:
        whole_state = jnp.where(
            take,
            whole_state + whole_gain[:, None] * got_state,
            got_state + got_gain[:, None] * whole_state,
        )
        whole_gain = whole_gain * got_gain
    return (part_gain, part_state, whole_gain, whole_state)


def dp_sum(terms, axis):
    count = lax.axis_size(axis)
    if count != terms.shape[0] or count & (count - 1):
        return lax.psum(terms, axis)
    place = lax.axis_index(axis)
    pairs = lambda k: [(i, i ^ k) for i in range(count)]
    got = [terms[place]] + [
        lax.ppermute(lax.dynamic_index_in_dim(terms, place ^ k, 0, False), axis, pairs(k))
        for k in range(1, count)
    ]
    total = got[0]
    for piece in got[1:]:
        total = total + piece
    back = jnp.stack([total] + [lax.ppermute(total, axis, pairs(k)) for k in range(1, count)])
    return jnp.take(back, jnp.arange(count) ^ place, axis=0)


def passed_along(block, axis, distance):
    devices = range(lax.axis_size(axis))
    route = [(i - distance, i) for i in devices if i - distance in devices]
    return lax.ppermute(block, axis, route)


def shift_pixels(values, shift_down, shift_right, row_width):
    pixel_count = values.shape[-1]
    offset = shift_down * row_width + shift_right
    padded = jnp.pad(values, [(0, 0)] * (values.ndim - 1) + [(row_width + 1, row_width + 1)])
    shifted = lax.slice_in_dim(
        padded, row_width + 1 + offset, row_width + 1 + offset + pixel_count, axis=values.ndim - 1
    )
    column = jnp.arange(pixel_count) % row_width + shift_right
    inside = (column >= 0) & (column < row_width)
    return jnp.where(inside, shifted, jnp.zeros_like(shifted))


def unfold(values, row_width):
    return jnp.concatenate([shift_pixels(values, a, b, row_width) for a, b in TAP_OFFSETS], axis=1)


def fold_taps(tap_grads, row_width):
    channels = tap_grads.shape[1] // 9
    accumulated = jnp.zeros((tap_grads.shape[0], channels, tap_grads.shape[2]), jnp.float32)
    for tap_index, (a, b) in enumerate(TAP_OFFSETS):
        piece = tap_grads[:, tap_index * channels : (tap_index + 1) * channels]
        accumulated = accumulated + shift_pixels(piece, -a, -b, row_width)
    return accumulated


def unfold_taps(squashed, row, column):
    pixels = squashed.shape[-1]
    pieces = []
    for down, right in TAP_OFFSETS:
        shift = down * WID + right
        moved = pltpu.roll(squashed, (-shift) % pixels, 1) if shift else squashed
        inside = (row + down >= 0) & (row + down < WID) & (column + right >= 0) & (column + right < WID)
        pieces.append(jnp.where(inside, moved, 0.0).astype(jnp.bfloat16))
    return jnp.concatenate(pieces, axis=0)


def pixel_grid(pixels):
    place = lax.broadcasted_iota(jnp.int32, (1, pixels), 1)
    return place // WID, place % WID


def block_kernel(step_size, state_ref, weight_ref, out_ref, kept_ref):
    current = state_ref[...]
    row, column = pixel_grid(current.shape[-1])
    for layer in range(weight_ref.shape[0]):
        kept_ref[layer] = current
        patches = unfold_taps(jnp.tanh(current), row, column)
        mixed = jnp.dot(weight_ref[layer], patches, preferred_element_type=jnp.float32)
        current = current + step_size * mixed
    out_ref[...] = current


def back_kernel(step_size, kept_ref, flipped_ref, upstream_ref, out_ref, grads_ref):
    upstream = upstream_ref[...]
    channels, pixels = upstream.shape
    row, column = pixel_grid(pixels)
    for layer in reversed(range(kept_ref.shape[0])):
        squashed = jnp.tanh(kept_ref[layer])
        patches = unfold_taps(squashed, row, column)
        scaled = (step_size * upstream).astype(jnp.bfloat16)
        grads_ref[layer] = lax.dot_general(
            scaled, patches, (((1,), (1,)), ((), ())), preferred_element_type=jnp.float32
        )
        spread = jnp.dot(flipped_ref[layer], scaled, preferred_element_type=jnp.float32)
        folded = jnp.zeros((channels, pixels), jnp.float32)
        for tap, (down, right) in enumerate(TAP_OFFSETS):
            shift = down * WID + right
            piece = spread[tap * channels : (tap + 1) * channels]
            moved = pltpu.roll(piece, shift % pixels, 1) if shift else piece
            inside = (row - down >= 0) & (row - down < WID) & (column - right >= 0) & (column - right < WID)
            folded = folded + jnp.where(inside, moved, 0.0)
        upstream = upstream + (1.0 - squashed * squashed) * folded
    out_ref[...] = upstream


def run_block(current, block_weights, step_size):
    layers, channels, pixels = block_weights.shape[0], current.shape[-2], current.shape[-1]
    spec = pl.BlockSpec(memory_space=pltpu.VMEM)
    out, kept = pl.pallas_call(
        functools.partial(block_kernel, step_size),
        out_shape=(
            jax.ShapeDtypeStruct((channels, pixels), jnp.float32),
            jax.ShapeDtypeStruct((layers, channels, pixels), jnp.float32),
        ),
        in_specs=[spec, spec],
        out_specs=(spec, spec),
        cost_estimate=pl.CostEstimate(
            flops=2 * layers * channels * block_weights.shape[-1] * pixels,
            transcendentals=layers * channels * pixels,
            bytes_accessed=4 * (layers + 2) * channels * pixels + 2 * block_weights.size,
        ),
    )(current.reshape(channels, pixels), block_weights)
    return (out.reshape(current.shape), [kept[k].reshape(current.shape) for k in range(layers)])


def back_block(inputs_kept, block_weights, upstream, step_size):
    layers, channels, pixels = block_weights.shape[0], upstream.shape[-2], upstream.shape[-1]
    taps = block_weights.shape[-1]
    flipped = jnp.swapaxes(block_weights, 1, 2)
    spec = pl.BlockSpec(memory_space=pltpu.VMEM)
    out, grads = pl.pallas_call(
        functools.partial(back_kernel, step_size),
        out_shape=(
            jax.ShapeDtypeStruct((channels, pixels), jnp.float32),
            jax.ShapeDtypeStruct((layers, channels, taps), jnp.float32),
        ),
        in_specs=[spec, spec, spec],
        out_specs=(spec, spec),
        cost_estimate=pl.CostEstimate(
            flops=4 * layers * channels * taps * pixels,
            transcendentals=layers * channels * pixels,
            bytes_accessed=4 * (layers + 2) * channels * pixels + 2 * block_weights.size + 4 * layers * channels * taps,
        ),
    )(jnp.stack(inputs_kept).reshape(layers, channels, pixels), flipped, upstream.reshape(channels, pixels))
    return (out.reshape(upstream.shape), grads)


def body(cpoints, weights, coarse_gain, cotangent):
    step_size = 1.0 / (weights.shape[0] * lax.axis_size("depth"))
    rounds = (lax.axis_size("depth") - 1).bit_length()
    place = lax.axis_index("depth")
    own_state = cpoints[0]
    rate_vec = coarse_gain[0]
    cot_here = cotangent[0]
    leading = place == 0

    def before(bit):
        return (place >> bit) % 2 == 1

    def after(bit):
        return (place >> bit) % 2 == 0

    relaxed, own_kept = run_block(own_state, weights, step_size)
    arriving = passed_along(relaxed, "depth", 1)
    start_state = jnp.where(leading, own_state, arriving)
    propagated, start_kept = run_block(start_state, weights, step_size)
    gained_start = rate_vec[None, :, None] * start_state
    offset = propagated - jnp.where(leading, jnp.zeros_like(gained_start), gained_start)
    forward = (rate_vec, offset, rate_vec, offset)
    reverse = (jnp.ones_like(rate_vec), jnp.zeros_like(cot_here), rate_vec, rate_vec[None, :, None] * cot_here)
    for bit in range(rounds):
        got_f, got_r = exchange(
            (forward[2], reverse[2]), jnp.stack([forward[3], reverse[3]]), "depth", bit
        )
        forward = scan_round(forward, got_f, before, bit, bit == rounds - 1)
        reverse = scan_round(reverse, got_r, after, bit, bit == rounds - 1)
    passed_in = reverse[1]
    adjoint_here = cot_here + passed_in
    back_start, start_grads = back_block(start_kept, weights, adjoint_here, step_size)
    arriving_bar = passed_along(back_start, "depth", -1)
    relaxed_bar = arriving_bar - passed_in
    back_own, own_grads = back_block(own_kept, weights, relaxed_bar, step_size)
    corrected = forward[1]
    grad_cpoints = jnp.where(leading, back_own + back_start, back_own)
    grad_weights = dp_sum(start_grads + own_grads, "dp")
    return (corrected[None], grad_cpoints[None], grad_weights)


def solution(mesh):
    placed = (
        P("depth", "dp", None, None),
        P("depth", None, None),
        P("depth", None),
        P("depth", "dp", None, None),
    )
    return jax.shard_map(
        body,
        mesh=mesh,
        in_specs=placed,
        out_specs=(
            P("depth", "dp", None, None),
            P("depth", "dp", None, None),
            P("depth", None, None),
        ),
        check_vma=False,
    )
```

```python
import functools

import jax
import jax.numpy as jnp
from jax import lax
from jax.sharding import PartitionSpec as P
from jax.experimental import pallas as pl
from jax.experimental.pallas import tpu as pltpu

WID = 16


TAP_OFFSETS = [(-1, -1), (-1, 0), (-1, 1), (0, -1), (0, 0), (0, 1), (1, -1), (1, 0), (1, 1)]


def pack(gains, states):
    width = states.shape[-1]
    rows = [jnp.pad(g, (0, width - g.shape[0]))[None] for g in gains]
    return jnp.concatenate([states.reshape(-1, width)] + rows, axis=0)


def exchange(gains, states, axis, mask):
    count = lax.axis_size(axis)
    arrived = lax.ppermute(pack(gains, states), axis, [(i, i ^ mask) for i in range(count)])
    rows = states.size // states.shape[-1]
    each = states.shape[1:]
    got = arrived[:rows].reshape(states.shape)
    return tuple(
        (arrived[rows + k, : g.shape[0]], got[k].reshape(each)) for k, g in enumerate(gains)
    )


def scan_round(scan, arrived, partner_first, bit, last):
    part_gain, part_state, whole_gain, whole_state = scan
    got_gain, got_state = arrived
    take = partner_first(bit)
    part_state = jnp.where(take, part_state + part_gain[:, None] * got_state, part_state)
    part_gain = jnp.where(take, part_gain * got_gain, part_gain)
    if not last:
        whole_state = jnp.where(
            take,
            whole_state + whole_gain[:, None] * got_state,
            got_state + got_gain[:, None] * whole_state,
        )
        whole_gain = whole_gain * got_gain
    return (part_gain, part_state, whole_gain, whole_state)


def dp_sum(terms, axis):
    count = lax.axis_size(axis)
    if count != terms.shape[0] or count & (count - 1):
        return lax.psum(terms, axis)
    place = lax.axis_index(axis)
    pairs = lambda k: [(i, i ^ k) for i in range(count)]
    got = [terms[place]] + [
        lax.ppermute(lax.dynamic_index_in_dim(terms, place ^ k, 0, False), axis, pairs(k))
        for k in range(1, count)
    ]
    total = got[0]
    for piece in got[1:]:
        total = total + piece
    back = jnp.stack([total] + [lax.ppermute(total, axis, pairs(k)) for k in range(1, count)])
    return jnp.take(back, jnp.arange(count) ^ place, axis=0)


def passed_along(block, axis, distance):
    devices = range(lax.axis_size(axis))
    route = [(i - distance, i) for i in devices if i - distance in devices]
    return lax.ppermute(block, axis, route)


def shift_pixels(values, shift_down, shift_right, row_width):
    pixel_count = values.shape[-1]
    offset = shift_down * row_width + shift_right
    padded = jnp.pad(values, [(0, 0)] * (values.ndim - 1) + [(row_width + 1, row_width + 1)])
    shifted = lax.slice_in_dim(
        padded, row_width + 1 + offset, row_width + 1 + offset + pixel_count, axis=values.ndim - 1
    )
    column = jnp.arange(pixel_count) % row_width + shift_right
    inside = (column >= 0) & (column < row_width)
    return jnp.where(inside, shifted, jnp.zeros_like(shifted))


def unfold(values, row_width):
    return jnp.concatenate([shift_pixels(values, a, b, row_width) for a, b in TAP_OFFSETS], axis=1)


def fold_taps(tap_grads, row_width):
    channels = tap_grads.shape[1] // 9
    accumulated = jnp.zeros((tap_grads.shape[0], channels, tap_grads.shape[2]), jnp.float32)
    for tap_index, (a, b) in enumerate(TAP_OFFSETS):
        piece = tap_grads[:, tap_index * channels : (tap_index + 1) * channels]
        accumulated = accumulated + shift_pixels(piece, -a, -b, row_width)
    return accumulated


def unfold_taps(squashed, row, column):
    pixels = squashed.shape[-1]
    pieces = []
    for down, right in TAP_OFFSETS:
        shift = down * WID + right
        moved = pltpu.roll(squashed, (-shift) % pixels, 1) if shift else squashed
        inside = (row + down >= 0) & (row + down < WID) & (column + right >= 0) & (column + right < WID)
        pieces.append(jnp.where(inside, moved, 0.0).astype(jnp.bfloat16))
    return jnp.concatenate(pieces, axis=0)


def pixel_grid(pixels):
    place = lax.broadcasted_iota(jnp.int32, (1, pixels), 1)
    return place // WID, place % WID


def block_kernel(step_size, state_ref, weight_ref, out_ref, kept_ref):
    current = state_ref[...]
    row, column = pixel_grid(current.shape[-1])
    for layer in range(weight_ref.shape[0]):
        kept_ref[layer] = current
        patches = unfold_taps(jnp.tanh(current), row, column)
        mixed = jnp.dot(weight_ref[layer], patches, preferred_element_type=jnp.float32)
        current = current + step_size * mixed
    out_ref[...] = current


def back_kernel(step_size, kept_ref, flipped_ref, upstream_ref, out_ref, grads_ref):
    upstream = upstream_ref[...]
    channels, pixels = upstream.shape
    row, column = pixel_grid(pixels)
    for layer in reversed(range(kept_ref.shape[0])):
        squashed = jnp.tanh(kept_ref[layer])
        patches = unfold_taps(squashed, row, column)
        scaled = (step_size * upstream).astype(jnp.bfloat16)
        grads_ref[layer] = lax.dot_general(
            scaled, patches, (((1,), (1,)), ((), ())), preferred_element_type=jnp.float32
        )
        spread = jnp.dot(flipped_ref[layer], scaled, preferred_element_type=jnp.float32)
        folded = jnp.zeros((channels, pixels), jnp.float32)
        for tap, (down, right) in enumerate(TAP_OFFSETS):
            shift = down * WID + right
            piece = spread[tap * channels : (tap + 1) * channels]
            moved = pltpu.roll(piece, shift % pixels, 1) if shift else piece
            inside = (row - down >= 0) & (row - down < WID) & (column - right >= 0) & (column - right < WID)
            folded = folded + jnp.where(inside, moved, 0.0)
        upstream = upstream + (1.0 - squashed * squashed) * folded
    out_ref[...] = upstream


def run_block(current, block_weights, step_size):
    layers, channels, pixels = block_weights.shape[0], current.shape[-2], current.shape[-1]
    spec = pl.BlockSpec(memory_space=pltpu.VMEM)
    out, kept = pl.pallas_call(
        functools.partial(block_kernel, step_size),
        out_shape=(
            jax.ShapeDtypeStruct((channels, pixels), jnp.float32),
            jax.ShapeDtypeStruct((layers, channels, pixels), jnp.float32),
        ),
        in_specs=[spec, spec],
        out_specs=(spec, spec),
        cost_estimate=pl.CostEstimate(
            flops=2 * layers * channels * block_weights.shape[-1] * pixels,
            transcendentals=layers * channels * pixels,
            bytes_accessed=4 * (layers + 2) * channels * pixels + 2 * block_weights.size,
        ),
    )(current.reshape(channels, pixels), block_weights)
    return (out.reshape(current.shape), [kept[k].reshape(current.shape) for k in range(layers)])


def back_block(inputs_kept, block_weights, upstream, step_size):
    layers, channels, pixels = block_weights.shape[0], upstream.shape[-2], upstream.shape[-1]
    taps = block_weights.shape[-1]
    flipped = jnp.swapaxes(block_weights, 1, 2)
    spec = pl.BlockSpec(memory_space=pltpu.VMEM)
    out, grads = pl.pallas_call(
        functools.partial(back_kernel, step_size),
        out_shape=(
            jax.ShapeDtypeStruct((channels, pixels), jnp.float32),
            jax.ShapeDtypeStruct((layers, channels, taps), jnp.float32),
        ),
        in_specs=[spec, spec, spec],
        out_specs=(spec, spec),
        cost_estimate=pl.CostEstimate(
            flops=4 * layers * channels * taps * pixels,
            transcendentals=layers * channels * pixels,
            bytes_accessed=4 * (layers + 2) * channels * pixels + 2 * block_weights.size + 4 * layers * channels * taps,
        ),
    )(jnp.stack(inputs_kept).reshape(layers, channels, pixels), flipped, upstream.reshape(channels, pixels))
    return (out.reshape(upstream.shape), grads)


def body(cpoints, weights, coarse_gain, cotangent):
    step_size = 1.0 / (weights.shape[0] * lax.axis_size("depth"))
    rounds = (lax.axis_size("depth") - 1).bit_length()
    place = lax.axis_index("depth")
    own_state = cpoints[0]
    rate_vec = coarse_gain[0]
    cot_here = cotangent[0]
    leading = place == 0

    def before(bit):
        return (place >> bit) % 2 == 1

    def after(bit):
        return (place >> bit) % 2 == 0

    relaxed, own_kept = run_block(own_state, weights, step_size)
    arriving = passed_along(relaxed, "depth", 1)
    start_state = jnp.where(leading, own_state, arriving)
    propagated, start_kept = run_block(start_state, weights, step_size)
    gained_start = rate_vec[None, :, None] * start_state
    offset = propagated - jnp.where(leading, jnp.zeros_like(gained_start), gained_start)
    forward = (rate_vec, offset, rate_vec, offset)
    reverse = (jnp.ones_like(rate_vec), jnp.zeros_like(cot_here), rate_vec, rate_vec[None, :, None] * cot_here)
    for bit in range(rounds):
        mask = 3 << (bit - 1) if bit == rounds - 1 and bit >= 1 else 1 << bit
        got_f, got_r = exchange(
            (forward[2], reverse[2]), jnp.stack([forward[3], reverse[3]]), "depth", mask
        )
        forward = scan_round(forward, got_f, before, bit, bit == rounds - 1)
        reverse = scan_round(reverse, got_r, after, bit, bit == rounds - 1)
    passed_in = reverse[1]
    adjoint_here = cot_here + passed_in
    back_start, start_grads = back_block(start_kept, weights, adjoint_here, step_size)
    arriving_bar = passed_along(back_start, "depth", -1)
    relaxed_bar = arriving_bar - passed_in
    back_own, own_grads = back_block(own_kept, weights, relaxed_bar, step_size)
    corrected = forward[1]
    grad_cpoints = jnp.where(leading, back_own + back_start, back_own)
    grad_weights = dp_sum(start_grads + own_grads, "dp")
    return (corrected[None], grad_cpoints[None], grad_weights)


def solution(mesh):
    placed = (
        P("depth", "dp", None, None),
        P("depth", None, None),
        P("depth", None),
        P("depth", "dp", None, None),
    )
    return jax.shard_map(
        body,
        mesh=mesh,
        in_specs=placed,
        out_specs=(
            P("depth", "dp", None, None),
            P("depth", "dp", None, None),
            P("depth", None, None),
        ),
        check_vma=False,
    )
```

```python
import functools

import jax
import jax.numpy as jnp
from jax import lax
from jax.sharding import PartitionSpec as P
from jax.experimental import pallas as pl
from jax.experimental.pallas import tpu as pltpu

WID = 16


TAP_OFFSETS = [(-1, -1), (-1, 0), (-1, 1), (0, -1), (0, 0), (0, 1), (1, -1), (1, 0), (1, 1)]


def pack(gains, states):
    width = states.shape[-1]
    rows = [jnp.pad(g, (0, width - g.shape[0]))[None] for g in gains]
    return jnp.concatenate([states.reshape(-1, width)] + rows, axis=0)


def exchange(gains, states, axis, mask):
    count = lax.axis_size(axis)
    arrived = lax.ppermute(pack(gains, states), axis, [(i, i ^ mask) for i in range(count)])
    rows = states.size // states.shape[-1]
    each = states.shape[1:]
    got = arrived[:rows].reshape(states.shape)
    return tuple(
        (arrived[rows + k, : g.shape[0]], got[k].reshape(each)) for k, g in enumerate(gains)
    )


def scan_round(scan, arrived, partner_first, bit, last):
    part_gain, part_state, whole_gain, whole_state = scan
    got_gain, got_state = arrived
    take = partner_first(bit)
    part_state = jnp.where(take, part_state + part_gain[:, None] * got_state, part_state)
    part_gain = jnp.where(take, part_gain * got_gain, part_gain)
    if not last:
        whole_state = jnp.where(
            take,
            whole_state + whole_gain[:, None] * got_state,
            got_state + got_gain[:, None] * whole_state,
        )
        whole_gain = whole_gain * got_gain
    return (part_gain, part_state, whole_gain, whole_state)


def dp_sum(terms, axis):
    count = lax.axis_size(axis)
    if count != terms.shape[0] or count & (count - 1):
        return lax.psum(terms, axis)
    place = lax.axis_index(axis)
    pairs = lambda k: [(i, i ^ k) for i in range(count)]
    got = [terms[place]] + [
        lax.ppermute(lax.dynamic_index_in_dim(terms, place ^ k, 0, False), axis, pairs(k))
        for k in range(1, count)
    ]
    total = got[0]
    for piece in got[1:]:
        total = total + piece
    back = jnp.stack([total] + [lax.ppermute(total, axis, pairs(k)) for k in range(1, count)])
    return jnp.take(back, jnp.arange(count) ^ place, axis=0)


def passed_along(block, axis, distance):
    devices = range(lax.axis_size(axis))
    route = [(i - distance, i) for i in devices if i - distance in devices]
    return lax.ppermute(block, axis, route)


def shift_pixels(values, shift_down, shift_right, row_width):
    pixel_count = values.shape[-1]
    offset = shift_down * row_width + shift_right
    padded = jnp.pad(values, [(0, 0)] * (values.ndim - 1) + [(row_width + 1, row_width + 1)])
    shifted = lax.slice_in_dim(
        padded, row_width + 1 + offset, row_width + 1 + offset + pixel_count, axis=values.ndim - 1
    )
    column = jnp.arange(pixel_count) % row_width + shift_right
    inside = (column >= 0) & (column < row_width)
    return jnp.where(inside, shifted, jnp.zeros_like(shifted))


def unfold(values, row_width):
    return jnp.concatenate([shift_pixels(values, a, b, row_width) for a, b in TAP_OFFSETS], axis=1)


def fold_taps(tap_grads, row_width):
    channels = tap_grads.shape[1] // 9
    accumulated = jnp.zeros((tap_grads.shape[0], channels, tap_grads.shape[2]), jnp.float32)
    for tap_index, (a, b) in enumerate(TAP_OFFSETS):
        piece = tap_grads[:, tap_index * channels : (tap_index + 1) * channels]
        accumulated = accumulated + shift_pixels(piece, -a, -b, row_width)
    return accumulated


def unfold_taps(squashed, row, column):
    pixels = squashed.shape[-1]
    pieces = []
    for down, right in TAP_OFFSETS:
        shift = down * WID + right
        moved = pltpu.roll(squashed, (-shift) % pixels, 1) if shift else squashed
        inside = (row + down >= 0) & (row + down < WID) & (column + right >= 0) & (column + right < WID)
        pieces.append(jnp.where(inside, moved, 0.0).astype(jnp.bfloat16))
    return jnp.concatenate(pieces, axis=0)


def pixel_grid(pixels):
    place = lax.broadcasted_iota(jnp.int32, (1, pixels), 1)
    return place // WID, place % WID


def block_kernel(step_size, state_ref, weight_ref, out_ref, kept_ref):
    current = state_ref[...]
    row, column = pixel_grid(current.shape[-1])
    for layer in range(weight_ref.shape[0]):
        kept_ref[layer] = current
        patches = unfold_taps(jnp.tanh(current), row, column)
        mixed = jnp.dot(weight_ref[layer], patches, preferred_element_type=jnp.float32)
        current = current + step_size * mixed
    out_ref[...] = current


def back_kernel(step_size, kept_ref, flipped_ref, upstream_ref, out_ref, grads_ref):
    upstream = upstream_ref[...]
    channels, pixels = upstream.shape
    row, column = pixel_grid(pixels)
    for layer in reversed(range(kept_ref.shape[0])):
        squashed = jnp.tanh(kept_ref[layer])
        patches = unfold_taps(squashed, row, column)
        scaled = (step_size * upstream).astype(jnp.bfloat16)
        grads_ref[layer] = lax.dot_general(
            scaled, patches, (((1,), (1,)), ((), ())), preferred_element_type=jnp.float32
        )
        spread = jnp.dot(flipped_ref[layer], scaled, preferred_element_type=jnp.float32)
        folded = jnp.zeros((channels, pixels), jnp.float32)
        for tap, (down, right) in enumerate(TAP_OFFSETS):
            shift = down * WID + right
            piece = spread[tap * channels : (tap + 1) * channels]
            moved = pltpu.roll(piece, shift % pixels, 1) if shift else piece
            inside = (row - down >= 0) & (row - down < WID) & (column - right >= 0) & (column - right < WID)
            folded = folded + jnp.where(inside, moved, 0.0)
        upstream = upstream + (1.0 - squashed * squashed) * folded
    out_ref[...] = upstream


def run_block(current, block_weights, step_size):
    layers, channels, pixels = block_weights.shape[0], current.shape[-2], current.shape[-1]
    spec = pl.BlockSpec(memory_space=pltpu.VMEM)
    out, kept = pl.pallas_call(
        functools.partial(block_kernel, step_size),
        out_shape=(
            jax.ShapeDtypeStruct((channels, pixels), jnp.float32),
            jax.ShapeDtypeStruct((layers, channels, pixels), jnp.float32),
        ),
        in_specs=[spec, spec],
        out_specs=(spec, spec),
        cost_estimate=pl.CostEstimate(
            flops=2 * layers * channels * block_weights.shape[-1] * pixels,
            transcendentals=layers * channels * pixels,
            bytes_accessed=4 * (layers + 2) * channels * pixels + 2 * block_weights.size,
        ),
    )(current.reshape(channels, pixels), block_weights)
    return (out.reshape(current.shape), [kept[k].reshape(current.shape) for k in range(layers)])


def back_block(inputs_kept, block_weights, upstream, step_size):
    layers, channels, pixels = block_weights.shape[0], upstream.shape[-2], upstream.shape[-1]
    taps = block_weights.shape[-1]
    flipped = jnp.swapaxes(block_weights, 1, 2)
    spec = pl.BlockSpec(memory_space=pltpu.VMEM)
    out, grads = pl.pallas_call(
        functools.partial(back_kernel, step_size),
        out_shape=(
            jax.ShapeDtypeStruct((channels, pixels), jnp.float32),
            jax.ShapeDtypeStruct((layers, channels, taps), jnp.float32),
        ),
        in_specs=[spec, spec, spec],
        out_specs=(spec, spec),
        cost_estimate=pl.CostEstimate(
            flops=4 * layers * channels * taps * pixels,
            transcendentals=layers * channels * pixels,
            bytes_accessed=4 * (layers + 2) * channels * pixels + 2 * block_weights.size + 4 * layers * channels * taps,
        ),
    )(jnp.stack(inputs_kept).reshape(layers, channels, pixels), flipped, upstream.reshape(channels, pixels))
    return (out.reshape(upstream.shape), grads)


def body(cpoints, weights, coarse_gain, cotangent):
    step_size = 1.0 / (weights.shape[0] * lax.axis_size("depth"))
    rounds = (lax.axis_size("depth") - 1).bit_length()
    place = lax.axis_index("depth")
    own_state = cpoints[0]
    rate_vec = coarse_gain[0]
    cot_here = cotangent[0]
    leading = place == 0

    def before(bit):
        return (place >> bit) % 2 == 1

    def after(bit):
        return (place >> bit) % 2 == 0

    relaxed, own_kept = run_block(own_state, weights, step_size)
    arriving = passed_along(relaxed, "depth", 1)
    start_state = jnp.where(leading, own_state, arriving)
    propagated, start_kept = run_block(start_state, weights, step_size)
    gained_start = rate_vec[None, :, None] * start_state
    offset = propagated - jnp.where(leading, jnp.zeros_like(gained_start), gained_start)
    forward = (rate_vec, offset, rate_vec, offset)
    reverse = (jnp.ones_like(rate_vec), jnp.zeros_like(cot_here), rate_vec, rate_vec[None, :, None] * cot_here)
    for bit in range(rounds):
        wide = {rounds - 1, 2} if rounds >= 4 else {rounds - 1}
        mask = 3 << (bit - 1) if bit in wide and bit >= 1 else 1 << bit
        got_f, got_r = exchange(
            (forward[2], reverse[2]), jnp.stack([forward[3], reverse[3]]), "depth", mask
        )
        forward = scan_round(forward, got_f, before, bit, bit == rounds - 1)
        reverse = scan_round(reverse, got_r, after, bit, bit == rounds - 1)
    passed_in = reverse[1]
    adjoint_here = cot_here + passed_in
    back_start, start_grads = back_block(start_kept, weights, adjoint_here, step_size)
    arriving_bar = passed_along(back_start, "depth", -1)
    relaxed_bar = arriving_bar - passed_in
    back_own, own_grads = back_block(own_kept, weights, relaxed_bar, step_size)
    corrected = forward[1]
    grad_cpoints = jnp.where(leading, back_own + back_start, back_own)
    grad_weights = dp_sum(start_grads + own_grads, "dp")
    return (corrected[None], grad_cpoints[None], grad_weights)


def solution(mesh):
    placed = (
        P("depth", "dp", None, None),
        P("depth", None, None),
        P("depth", None),
        P("depth", "dp", None, None),
    )
    return jax.shard_map(
        body,
        mesh=mesh,
        in_specs=placed,
        out_specs=(
            P("depth", "dp", None, None),
            P("depth", "dp", None, None),
            P("depth", None, None),
        ),
        check_vma=False,
    )
```

```python
import functools

import jax
import jax.numpy as jnp
from jax import lax
from jax.sharding import PartitionSpec as P
from jax.experimental import pallas as pl
from jax.experimental.pallas import tpu as pltpu

WID = 16


TAP_OFFSETS = [(-1, -1), (-1, 0), (-1, 1), (0, -1), (0, 0), (0, 1), (1, -1), (1, 0), (1, 1)]


def pack(gains, states):
    width = states.shape[-1]
    rows = [jnp.pad(g, (0, width - g.shape[0]))[None] for g in gains]
    return jnp.concatenate([states.reshape(-1, width)] + rows, axis=0)


def exchange(gains, states, axis, mask):
    count = lax.axis_size(axis)
    arrived = lax.ppermute(pack(gains, states), axis, [(i, i ^ mask) for i in range(count)])
    rows = states.size // states.shape[-1]
    each = states.shape[1:]
    got = arrived[:rows].reshape(states.shape)
    return tuple(
        (arrived[rows + k, : g.shape[0]], got[k].reshape(each)) for k, g in enumerate(gains)
    )


def scan_round(scan, arrived, partner_first, bit, last):
    part_gain, part_state, whole_gain, whole_state = scan
    got_gain, got_state = arrived
    take = partner_first(bit)
    part_state = jnp.where(take, part_state + part_gain[:, None] * got_state, part_state)
    part_gain = jnp.where(take, part_gain * got_gain, part_gain)
    if not last:
        whole_state = jnp.where(
            take,
            whole_state + whole_gain[:, None] * got_state,
            got_state + got_gain[:, None] * whole_state,
        )
        whole_gain = whole_gain * got_gain
    return (part_gain, part_state, whole_gain, whole_state)


def dp_sum(terms, axis):
    count = lax.axis_size(axis)
    if count != terms.shape[0]:
        return lax.psum(terms, axis)
    got = lax.all_to_all(terms, axis, 0, 0)
    total = got[0]
    for k in range(1, count):
        total = total + got[k]
    return lax.all_to_all(jnp.broadcast_to(total[None], terms.shape), axis, 0, 0)


def passed_along(block, axis, distance):
    devices = range(lax.axis_size(axis))
    route = [(i - distance, i) for i in devices if i - distance in devices]
    return lax.ppermute(block, axis, route)


def shift_pixels(values, shift_down, shift_right, row_width):
    pixel_count = values.shape[-1]
    offset = shift_down * row_width + shift_right
    padded = jnp.pad(values, [(0, 0)] * (values.ndim - 1) + [(row_width + 1, row_width + 1)])
    shifted = lax.slice_in_dim(
        padded, row_width + 1 + offset, row_width + 1 + offset + pixel_count, axis=values.ndim - 1
    )
    column = jnp.arange(pixel_count) % row_width + shift_right
    inside = (column >= 0) & (column < row_width)
    return jnp.where(inside, shifted, jnp.zeros_like(shifted))


def unfold(values, row_width):
    return jnp.concatenate([shift_pixels(values, a, b, row_width) for a, b in TAP_OFFSETS], axis=1)


def fold_taps(tap_grads, row_width):
    channels = tap_grads.shape[1] // 9
    accumulated = jnp.zeros((tap_grads.shape[0], channels, tap_grads.shape[2]), jnp.float32)
    for tap_index, (a, b) in enumerate(TAP_OFFSETS):
        piece = tap_grads[:, tap_index * channels : (tap_index + 1) * channels]
        accumulated = accumulated + shift_pixels(piece, -a, -b, row_width)
    return accumulated


def unfold_taps(squashed, row, column):
    pixels = squashed.shape[-1]
    pieces = []
    for down, right in TAP_OFFSETS:
        shift = down * WID + right
        moved = pltpu.roll(squashed, (-shift) % pixels, 1) if shift else squashed
        inside = (row + down >= 0) & (row + down < WID) & (column + right >= 0) & (column + right < WID)
        pieces.append(jnp.where(inside, moved, 0.0).astype(jnp.bfloat16))
    return jnp.concatenate(pieces, axis=0)


def pixel_grid(pixels):
    place = lax.broadcasted_iota(jnp.int32, (1, pixels), 1)
    return place // WID, place % WID


def block_kernel(step_size, state_ref, weight_ref, out_ref, kept_ref):
    current = state_ref[...]
    row, column = pixel_grid(current.shape[-1])
    for layer in range(weight_ref.shape[0]):
        kept_ref[layer] = current
        patches = unfold_taps(jnp.tanh(current), row, column)
        mixed = jnp.dot(weight_ref[layer], patches, preferred_element_type=jnp.float32)
        current = current + step_size * mixed
    out_ref[...] = current


def back_kernel(step_size, kept_ref, flipped_ref, upstream_ref, out_ref, grads_ref):
    upstream = upstream_ref[...]
    channels, pixels = upstream.shape
    row, column = pixel_grid(pixels)
    for layer in reversed(range(kept_ref.shape[0])):
        squashed = jnp.tanh(kept_ref[layer])
        patches = unfold_taps(squashed, row, column)
        scaled = (step_size * upstream).astype(jnp.bfloat16)
        grads_ref[layer] = lax.dot_general(
            scaled, patches, (((1,), (1,)), ((), ())), preferred_element_type=jnp.float32
        )
        spread = jnp.dot(flipped_ref[layer], scaled, preferred_element_type=jnp.float32)
        folded = jnp.zeros((channels, pixels), jnp.float32)
        for tap, (down, right) in enumerate(TAP_OFFSETS):
            shift = down * WID + right
            piece = spread[tap * channels : (tap + 1) * channels]
            moved = pltpu.roll(piece, shift % pixels, 1) if shift else piece
            inside = (row - down >= 0) & (row - down < WID) & (column - right >= 0) & (column - right < WID)
            folded = folded + jnp.where(inside, moved, 0.0)
        upstream = upstream + (1.0 - squashed * squashed) * folded
    out_ref[...] = upstream


def run_block(current, block_weights, step_size):
    layers, channels, pixels = block_weights.shape[0], current.shape[-2], current.shape[-1]
    spec = pl.BlockSpec(memory_space=pltpu.VMEM)
    out, kept = pl.pallas_call(
        functools.partial(block_kernel, step_size),
        out_shape=(
            jax.ShapeDtypeStruct((channels, pixels), jnp.float32),
            jax.ShapeDtypeStruct((layers, channels, pixels), jnp.float32),
        ),
        in_specs=[spec, spec],
        out_specs=(spec, spec),
        cost_estimate=pl.CostEstimate(
            flops=2 * layers * channels * block_weights.shape[-1] * pixels,
            transcendentals=layers * channels * pixels,
            bytes_accessed=4 * (layers + 2) * channels * pixels + 2 * block_weights.size,
        ),
    )(current.reshape(channels, pixels), block_weights)
    return (out.reshape(current.shape), [kept[k].reshape(current.shape) for k in range(layers)])


def back_block(inputs_kept, block_weights, upstream, step_size):
    layers, channels, pixels = block_weights.shape[0], upstream.shape[-2], upstream.shape[-1]
    taps = block_weights.shape[-1]
    flipped = jnp.swapaxes(block_weights, 1, 2)
    spec = pl.BlockSpec(memory_space=pltpu.VMEM)
    out, grads = pl.pallas_call(
        functools.partial(back_kernel, step_size),
        out_shape=(
            jax.ShapeDtypeStruct((channels, pixels), jnp.float32),
            jax.ShapeDtypeStruct((layers, channels, taps), jnp.float32),
        ),
        in_specs=[spec, spec, spec],
        out_specs=(spec, spec),
        cost_estimate=pl.CostEstimate(
            flops=4 * layers * channels * taps * pixels,
            transcendentals=layers * channels * pixels,
            bytes_accessed=4 * (layers + 2) * channels * pixels + 2 * block_weights.size + 4 * layers * channels * taps,
        ),
    )(jnp.stack(inputs_kept).reshape(layers, channels, pixels), flipped, upstream.reshape(channels, pixels))
    return (out.reshape(upstream.shape), grads)


def body(cpoints, weights, coarse_gain, cotangent):
    step_size = 1.0 / (weights.shape[0] * lax.axis_size("depth"))
    rounds = (lax.axis_size("depth") - 1).bit_length()
    place = lax.axis_index("depth")
    own_state = cpoints[0]
    rate_vec = coarse_gain[0]
    cot_here = cotangent[0]
    leading = place == 0

    def before(bit):
        return (place >> bit) % 2 == 1

    def after(bit):
        return (place >> bit) % 2 == 0

    relaxed, own_kept = run_block(own_state, weights, step_size)
    arriving = passed_along(relaxed, "depth", 1)
    start_state = jnp.where(leading, own_state, arriving)
    propagated, start_kept = run_block(start_state, weights, step_size)
    gained_start = rate_vec[None, :, None] * start_state
    offset = propagated - jnp.where(leading, jnp.zeros_like(gained_start), gained_start)
    forward = (rate_vec, offset, rate_vec, offset)
    reverse = (jnp.ones_like(rate_vec), jnp.zeros_like(cot_here), rate_vec, rate_vec[None, :, None] * cot_here)
    for bit in range(rounds):
        wide = {rounds - 1, 2} if rounds >= 4 else {rounds - 1}
        mask = 3 << (bit - 1) if bit in wide and bit >= 1 else 1 << bit
        got_f, got_r = exchange(
            (forward[2], reverse[2]), jnp.stack([forward[3], reverse[3]]), "depth", mask
        )
        forward = scan_round(forward, got_f, before, bit, bit == rounds - 1)
        reverse = scan_round(reverse, got_r, after, bit, bit == rounds - 1)
    passed_in = reverse[1]
    adjoint_here = cot_here + passed_in
    back_start, start_grads = back_block(start_kept, weights, adjoint_here, step_size)
    arriving_bar = passed_along(back_start, "depth", -1)
    relaxed_bar = arriving_bar - passed_in
    back_own, own_grads = back_block(own_kept, weights, relaxed_bar, step_size)
    corrected = forward[1]
    grad_cpoints = jnp.where(leading, back_own + back_start, back_own)
    grad_weights = dp_sum(start_grads + own_grads, "dp")
    return (corrected[None], grad_cpoints[None], grad_weights)


def solution(mesh):
    placed = (
        P("depth", "dp", None, None),
        P("depth", None, None),
        P("depth", None),
        P("depth", "dp", None, None),
    )
    return jax.shard_map(
        body,
        mesh=mesh,
        in_specs=placed,
        out_specs=(
            P("depth", "dp", None, None),
            P("depth", "dp", None, None),
            P("depth", None, None),
        ),
        check_vma=False,
    )
```

```python
import functools

import jax
import jax.numpy as jnp
from jax import lax
from jax.sharding import PartitionSpec as P
from jax.experimental import pallas as pl
from jax.experimental.pallas import tpu as pltpu

WID = 16


TAP_OFFSETS = [(-1, -1), (-1, 0), (-1, 1), (0, -1), (0, 0), (0, 1), (1, -1), (1, 0), (1, 1)]


def pack(gains, states):
    width = states.shape[-1]
    rows = [jnp.pad(g, (0, width - g.shape[0]))[None] for g in gains]
    return jnp.concatenate([states.reshape(-1, width)] + rows, axis=0)


def exchange(gains, states, axis, mask):
    count = lax.axis_size(axis)
    arrived = lax.ppermute(pack(gains, states), axis, [(i, i ^ mask) for i in range(count)])
    rows = states.size // states.shape[-1]
    each = states.shape[1:]
    got = arrived[:rows].reshape(states.shape)
    return tuple(
        (arrived[rows + k, : g.shape[0]], got[k].reshape(each)) for k, g in enumerate(gains)
    )


def scan_round(scan, arrived, partner_first, bit, last):
    part_gain, part_state, whole_gain, whole_state = scan
    got_gain, got_state = arrived
    take = partner_first(bit)
    part_state = jnp.where(take, part_state + part_gain[:, None] * got_state, part_state)
    part_gain = jnp.where(take, part_gain * got_gain, part_gain)
    if not last:
        whole_state = jnp.where(
            take,
            whole_state + whole_gain[:, None] * got_state,
            got_state + got_gain[:, None] * whole_state,
        )
        whole_gain = whole_gain * got_gain
    return (part_gain, part_state, whole_gain, whole_state)


def dp_sum(terms, axis):
    count = lax.axis_size(axis)
    if count != terms.shape[0] or count & (count - 1):
        return lax.psum(terms, axis)
    place = lax.axis_index(axis)
    pairs = lambda k: [(i, i ^ k) for i in range(count)]
    got = [terms[place]] + [
        lax.ppermute(lax.dynamic_index_in_dim(terms, place ^ k, 0, False), axis, pairs(k))
        for k in range(1, count)
    ]
    total = got[0]
    for piece in got[1:]:
        total = total + piece
    back = jnp.stack([total] + [lax.ppermute(total, axis, pairs(k)) for k in range(1, count)])
    return jnp.take(back, jnp.arange(count) ^ place, axis=0)


def passed_along(block, axis, distance):
    devices = range(lax.axis_size(axis))
    route = [(i - distance, i) for i in devices if i - distance in devices]
    return lax.ppermute(block, axis, route)


def shift_pixels(values, shift_down, shift_right, row_width):
    pixel_count = values.shape[-1]
    offset = shift_down * row_width + shift_right
    padded = jnp.pad(values, [(0, 0)] * (values.ndim - 1) + [(row_width + 1, row_width + 1)])
    shifted = lax.slice_in_dim(
        padded, row_width + 1 + offset, row_width + 1 + offset + pixel_count, axis=values.ndim - 1
    )
    column = jnp.arange(pixel_count) % row_width + shift_right
    inside = (column >= 0) & (column < row_width)
    return jnp.where(inside, shifted, jnp.zeros_like(shifted))


def unfold(values, row_width):
    return jnp.concatenate([shift_pixels(values, a, b, row_width) for a, b in TAP_OFFSETS], axis=1)


def fold_taps(tap_grads, row_width):
    channels = tap_grads.shape[1] // 9
    accumulated = jnp.zeros((tap_grads.shape[0], channels, tap_grads.shape[2]), jnp.float32)
    for tap_index, (a, b) in enumerate(TAP_OFFSETS):
        piece = tap_grads[:, tap_index * channels : (tap_index + 1) * channels]
        accumulated = accumulated + shift_pixels(piece, -a, -b, row_width)
    return accumulated


def unfold_taps(squashed, row, column):
    pixels = squashed.shape[-1]
    pieces = []
    for down, right in TAP_OFFSETS:
        shift = down * WID + right
        moved = pltpu.roll(squashed, (-shift) % pixels, 1) if shift else squashed
        inside = (row + down >= 0) & (row + down < WID) & (column + right >= 0) & (column + right < WID)
        pieces.append(jnp.where(inside, moved, 0.0).astype(jnp.bfloat16))
    return jnp.concatenate(pieces, axis=0)


def pixel_grid(pixels):
    place = lax.broadcasted_iota(jnp.int32, (1, pixels), 1)
    return place // WID, place % WID


def block_kernel(step_size, state_ref, weight_ref, out_ref, squashed_ref, patches_ref):
    current = state_ref[...]
    row, column = pixel_grid(current.shape[-1])
    for layer in range(weight_ref.shape[0]):
        squashed = jnp.tanh(current)
        patches = unfold_taps(squashed, row, column)
        squashed_ref[layer] = squashed
        patches_ref[layer] = patches
        mixed = jnp.dot(weight_ref[layer], patches, preferred_element_type=jnp.float32)
        current = current + step_size * mixed
    out_ref[...] = current


def back_kernel(step_size, squashed_ref, patches_ref, flipped_ref, upstream_ref, earlier_ref, out_ref, grads_ref):
    upstream = upstream_ref[...]
    channels, pixels = upstream.shape
    row, column = pixel_grid(pixels)
    for layer in reversed(range(squashed_ref.shape[0])):
        squashed = squashed_ref[layer]
        scaled = (step_size * upstream).astype(jnp.bfloat16)
        grads_ref[layer] = earlier_ref[layer] + lax.dot_general(
            scaled, patches_ref[layer], (((1,), (1,)), ((), ())), preferred_element_type=jnp.float32
        )
        spread = jnp.dot(flipped_ref[layer], scaled, preferred_element_type=jnp.float32)
        folded = jnp.zeros((channels, pixels), jnp.float32)
        for tap, (down, right) in enumerate(TAP_OFFSETS):
            shift = down * WID + right
            piece = spread[tap * channels : (tap + 1) * channels]
            moved = pltpu.roll(piece, shift % pixels, 1) if shift else piece
            inside = (row - down >= 0) & (row - down < WID) & (column - right >= 0) & (column - right < WID)
            folded = folded + jnp.where(inside, moved, 0.0)
        upstream = upstream + (1.0 - squashed * squashed) * folded
    out_ref[...] = upstream


def run_block(current, block_weights, step_size):
    layers, channels, pixels = block_weights.shape[0], current.shape[-2], current.shape[-1]
    taps = block_weights.shape[-1]
    spec = pl.BlockSpec(memory_space=pltpu.VMEM)
    out, squashed, patches = pl.pallas_call(
        functools.partial(block_kernel, step_size),
        out_shape=(
            jax.ShapeDtypeStruct((channels, pixels), jnp.float32),
            jax.ShapeDtypeStruct((layers, channels, pixels), jnp.float32),
            jax.ShapeDtypeStruct((layers, taps, pixels), jnp.bfloat16),
        ),
        in_specs=[spec, spec],
        out_specs=(spec, spec, spec),
        cost_estimate=pl.CostEstimate(
            flops=2 * layers * channels * taps * pixels,
            transcendentals=layers * channels * pixels,
            bytes_accessed=4 * (layers + 2) * channels * pixels + 2 * block_weights.size + 2 * layers * taps * pixels,
        ),
    )(current.reshape(channels, pixels), block_weights)
    return (out.reshape(current.shape), (squashed, patches))


def back_block(inputs_kept, block_weights, upstream, step_size, earlier=None):
    squashed, patches = inputs_kept
    layers, channels, pixels = block_weights.shape[0], upstream.shape[-2], upstream.shape[-1]
    taps = block_weights.shape[-1]
    if earlier is None:
        earlier = jnp.zeros((layers, channels, taps), jnp.float32)
    flipped = jnp.swapaxes(block_weights, 1, 2)
    spec = pl.BlockSpec(memory_space=pltpu.VMEM)
    out, grads = pl.pallas_call(
        functools.partial(back_kernel, step_size),
        out_shape=(
            jax.ShapeDtypeStruct((channels, pixels), jnp.float32),
            jax.ShapeDtypeStruct((layers, channels, taps), jnp.float32),
        ),
        in_specs=[spec] * 5,
        out_specs=(spec, spec),
        cost_estimate=pl.CostEstimate(
            flops=4 * layers * channels * taps * pixels,
            transcendentals=0,
            bytes_accessed=4 * (layers + 2) * channels * pixels + 2 * block_weights.size
            + 2 * layers * taps * pixels + 8 * layers * channels * taps,
        ),
    )(squashed, patches, flipped, upstream.reshape(channels, pixels), earlier)
    return (out.reshape(upstream.shape), grads)


def body(cpoints, weights, coarse_gain, cotangent):
    step_size = 1.0 / (weights.shape[0] * lax.axis_size("depth"))
    rounds = (lax.axis_size("depth") - 1).bit_length()
    place = lax.axis_index("depth")
    own_state = cpoints[0]
    rate_vec = coarse_gain[0]
    cot_here = cotangent[0]
    leading = place == 0

    def before(bit):
        return (place >> bit) % 2 == 1

    def after(bit):
        return (place >> bit) % 2 == 0

    relaxed, own_kept = run_block(own_state, weights, step_size)
    arriving = passed_along(relaxed, "depth", 1)
    start_state = jnp.where(leading, own_state, arriving)
    propagated, start_kept = run_block(start_state, weights, step_size)
    gained_start = rate_vec[None, :, None] * start_state
    offset = propagated - jnp.where(leading, jnp.zeros_like(gained_start), gained_start)
    forward = (rate_vec, offset, rate_vec, offset)
    reverse = (jnp.ones_like(rate_vec), jnp.zeros_like(cot_here), rate_vec, rate_vec[None, :, None] * cot_here)
    for bit in range(rounds):
        wide = {rounds - 1, 2} if rounds >= 4 else {rounds - 1}
        mask = 3 << (bit - 1) if bit in wide and bit >= 1 else 1 << bit
        got_f, got_r = exchange(
            (forward[2], reverse[2]), jnp.stack([forward[3], reverse[3]]), "depth", mask
        )
        forward = scan_round(forward, got_f, before, bit, bit == rounds - 1)
        reverse = scan_round(reverse, got_r, after, bit, bit == rounds - 1)
    passed_in = reverse[1]
    adjoint_here = cot_here + passed_in
    back_start, start_grads = back_block(start_kept, weights, adjoint_here, step_size)
    arriving_bar = passed_along(back_start, "depth", -1)
    relaxed_bar = arriving_bar - passed_in
    back_own, both_grads = back_block(own_kept, weights, relaxed_bar, step_size, start_grads)
    corrected = forward[1]
    grad_cpoints = jnp.where(leading, back_own + back_start, back_own)
    grad_weights = dp_sum(both_grads, "dp")
    return (corrected[None], grad_cpoints[None], grad_weights)


def solution(mesh):
    placed = (
        P("depth", "dp", None, None),
        P("depth", None, None),
        P("depth", None),
        P("depth", "dp", None, None),
    )
    return jax.shard_map(
        body,
        mesh=mesh,
        in_specs=placed,
        out_specs=(
            P("depth", "dp", None, None),
            P("depth", "dp", None, None),
            P("depth", None, None),
        ),
        check_vma=False,
    )
```

```python
import functools

import jax
import jax.numpy as jnp
from jax import lax
from jax.sharding import PartitionSpec as P
from jax.experimental import pallas as pl
from jax.experimental.pallas import tpu as pltpu

WID = 16


TAP_OFFSETS = [(-1, -1), (-1, 0), (-1, 1), (0, -1), (0, 0), (0, 1), (1, -1), (1, 0), (1, 1)]


def pack(gains, states):
    width = states.shape[-1]
    rows = [jnp.pad(g, (0, width - g.shape[0]))[None] for g in gains]
    return jnp.concatenate([states.reshape(-1, width)] + rows, axis=0)


def exchange(gains, states, axis, mask):
    count = lax.axis_size(axis)
    arrived = lax.ppermute(pack(gains, states), axis, [(i, i ^ mask) for i in range(count)])
    rows = states.size // states.shape[-1]
    each = states.shape[1:]
    got = arrived[:rows].reshape(states.shape)
    return tuple(
        (arrived[rows + k, : g.shape[0]], got[k].reshape(each)) for k, g in enumerate(gains)
    )


def scan_round(scan, arrived, partner_first, bit, last):
    part_gain, part_state, whole_gain, whole_state = scan
    got_gain, got_state = arrived
    take = partner_first(bit)
    part_state = jnp.where(take, part_state + part_gain[:, None] * got_state, part_state)
    part_gain = jnp.where(take, part_gain * got_gain, part_gain)
    if not last:
        whole_state = jnp.where(
            take,
            whole_state + whole_gain[:, None] * got_state,
            got_state + got_gain[:, None] * whole_state,
        )
        whole_gain = whole_gain * got_gain
    return (part_gain, part_state, whole_gain, whole_state)


def dp_sum(terms, axis):
    count = lax.axis_size(axis)
    if count != terms.shape[0] or count & (count - 1):
        return lax.psum(terms, axis)
    place = lax.axis_index(axis)
    pairs = lambda k: [(i, i ^ k) for i in range(count)]
    got = [terms[place]] + [
        lax.ppermute(lax.dynamic_index_in_dim(terms, place ^ k, 0, False), axis, pairs(k))
        for k in range(1, count)
    ]
    total = got[0]
    for piece in got[1:]:
        total = total + piece
    back = jnp.stack([total] + [lax.ppermute(total, axis, pairs(k)) for k in range(1, count)])
    return jnp.take(back, jnp.arange(count) ^ place, axis=0)


def passed_along(block, axis, distance):
    devices = range(lax.axis_size(axis))
    route = [(i - distance, i) for i in devices if i - distance in devices]
    return lax.ppermute(block, axis, route)


def shift_pixels(values, shift_down, shift_right, row_width):
    pixel_count = values.shape[-1]
    offset = shift_down * row_width + shift_right
    padded = jnp.pad(values, [(0, 0)] * (values.ndim - 1) + [(row_width + 1, row_width + 1)])
    shifted = lax.slice_in_dim(
        padded, row_width + 1 + offset, row_width + 1 + offset + pixel_count, axis=values.ndim - 1
    )
    column = jnp.arange(pixel_count) % row_width + shift_right
    inside = (column >= 0) & (column < row_width)
    return jnp.where(inside, shifted, jnp.zeros_like(shifted))


def unfold(values, row_width):
    return jnp.concatenate([shift_pixels(values, a, b, row_width) for a, b in TAP_OFFSETS], axis=1)


def fold_taps(tap_grads, row_width):
    channels = tap_grads.shape[1] // 9
    accumulated = jnp.zeros((tap_grads.shape[0], channels, tap_grads.shape[2]), jnp.float32)
    for tap_index, (a, b) in enumerate(TAP_OFFSETS):
        piece = tap_grads[:, tap_index * channels : (tap_index + 1) * channels]
        accumulated = accumulated + shift_pixels(piece, -a, -b, row_width)
    return accumulated


def unfold_taps(squashed, row, column):
    pixels = squashed.shape[-1]
    pieces = []
    for down, right in TAP_OFFSETS:
        shift = down * WID + right
        moved = pltpu.roll(squashed, (-shift) % pixels, 1) if shift else squashed
        inside = (row + down >= 0) & (row + down < WID) & (column + right >= 0) & (column + right < WID)
        pieces.append(jnp.where(inside, moved, 0.0).astype(jnp.bfloat16))
    return jnp.concatenate(pieces, axis=0)


def pixel_grid(pixels):
    place = lax.broadcasted_iota(jnp.int32, (1, pixels), 1)
    return place // WID, place % WID


def block_kernel(step_size, state_ref, weight_ref, out_ref, kept_ref):
    current = state_ref[...]
    row, column = pixel_grid(current.shape[-1])
    for layer in range(weight_ref.shape[0]):
        kept_ref[layer] = current
        patches = unfold_taps(jnp.tanh(current), row, column)
        mixed = jnp.dot(weight_ref[layer], patches, preferred_element_type=jnp.float32)
        current = current + step_size * mixed
    out_ref[...] = current


def back_kernel(step_size, kept_ref, flipped_ref, upstream_ref, earlier_ref, out_ref, grads_ref):
    upstream = upstream_ref[...]
    channels, pixels = upstream.shape
    row, column = pixel_grid(pixels)
    for layer in reversed(range(kept_ref.shape[0])):
        squashed = jnp.tanh(kept_ref[layer])
        patches = unfold_taps(squashed, row, column)
        scaled = (step_size * upstream).astype(jnp.bfloat16)
        grads_ref[layer] = earlier_ref[layer] + lax.dot_general(
            scaled, patches, (((1,), (1,)), ((), ())), preferred_element_type=jnp.float32
        )
        spread = jnp.dot(flipped_ref[layer], scaled, preferred_element_type=jnp.float32)
        folded = jnp.zeros((channels, pixels), jnp.float32)
        for tap, (down, right) in enumerate(TAP_OFFSETS):
            shift = down * WID + right
            piece = spread[tap * channels : (tap + 1) * channels]
            moved = pltpu.roll(piece, shift % pixels, 1) if shift else piece
            inside = (row - down >= 0) & (row - down < WID) & (column - right >= 0) & (column - right < WID)
            folded = folded + jnp.where(inside, moved, 0.0)
        upstream = upstream + (1.0 - squashed * squashed) * folded
    out_ref[...] = upstream


def run_block(current, block_weights, step_size):
    layers, channels, pixels = block_weights.shape[0], current.shape[-2], current.shape[-1]
    spec = pl.BlockSpec(memory_space=pltpu.VMEM)
    out, kept = pl.pallas_call(
        functools.partial(block_kernel, step_size),
        out_shape=(
            jax.ShapeDtypeStruct((channels, pixels), jnp.float32),
            jax.ShapeDtypeStruct((layers, channels, pixels), jnp.float32),
        ),
        in_specs=[spec, spec],
        out_specs=(spec, spec),
        cost_estimate=pl.CostEstimate(
            flops=2 * layers * channels * block_weights.shape[-1] * pixels,
            transcendentals=layers * channels * pixels,
            bytes_accessed=4 * (layers + 2) * channels * pixels + 2 * block_weights.size,
        ),
    )(current.reshape(channels, pixels), block_weights)
    return (out.reshape(current.shape), [kept[k].reshape(current.shape) for k in range(layers)])


def back_block(inputs_kept, block_weights, upstream, step_size, earlier=None):
    layers, channels, pixels = block_weights.shape[0], upstream.shape[-2], upstream.shape[-1]
    taps = block_weights.shape[-1]
    if earlier is None:
        earlier = jnp.zeros((layers, channels, taps), jnp.float32)
    flipped = jnp.swapaxes(block_weights, 1, 2)
    spec = pl.BlockSpec(memory_space=pltpu.VMEM)
    out, grads = pl.pallas_call(
        functools.partial(back_kernel, step_size),
        out_shape=(
            jax.ShapeDtypeStruct((channels, pixels), jnp.float32),
            jax.ShapeDtypeStruct((layers, channels, taps), jnp.float32),
        ),
        in_specs=[spec] * 4,
        out_specs=(spec, spec),
        cost_estimate=pl.CostEstimate(
            flops=4 * layers * channels * taps * pixels,
            transcendentals=layers * channels * pixels,
            bytes_accessed=4 * (layers + 2) * channels * pixels + 2 * block_weights.size + 4 * layers * channels * taps,
        ),
    )(jnp.stack(inputs_kept).reshape(layers, channels, pixels), flipped, upstream.reshape(channels, pixels), earlier)
    return (out.reshape(upstream.shape), grads)


def body(cpoints, weights, coarse_gain, cotangent):
    step_size = 1.0 / (weights.shape[0] * lax.axis_size("depth"))
    rounds = (lax.axis_size("depth") - 1).bit_length()
    place = lax.axis_index("depth")
    own_state = cpoints[0]
    rate_vec = coarse_gain[0]
    cot_here = cotangent[0]
    leading = place == 0

    def before(bit):
        return (place >> bit) % 2 == 1

    def after(bit):
        return (place >> bit) % 2 == 0

    relaxed, own_kept = run_block(own_state, weights, step_size)
    arriving = passed_along(relaxed, "depth", 1)
    start_state = jnp.where(leading, own_state, arriving)
    propagated, start_kept = run_block(start_state, weights, step_size)
    gained_start = rate_vec[None, :, None] * start_state
    offset = propagated - jnp.where(leading, jnp.zeros_like(gained_start), gained_start)
    forward = (rate_vec, offset, rate_vec, offset)
    reverse = (jnp.ones_like(rate_vec), jnp.zeros_like(cot_here), rate_vec, rate_vec[None, :, None] * cot_here)
    for bit in range(rounds):
        wide = {rounds - 1, 2} if rounds >= 4 else {rounds - 1}
        mask = 3 << (bit - 1) if bit in wide and bit >= 1 else 1 << bit
        got_f, got_r = exchange(
            (forward[2], reverse[2]), jnp.stack([forward[3], reverse[3]]), "depth", mask
        )
        forward = scan_round(forward, got_f, before, bit, bit == rounds - 1)
        reverse = scan_round(reverse, got_r, after, bit, bit == rounds - 1)
    passed_in = reverse[1]
    adjoint_here = cot_here + passed_in
    back_start, start_grads = back_block(start_kept, weights, adjoint_here, step_size)
    arriving_bar = passed_along(back_start, "depth", -1)
    relaxed_bar = arriving_bar - passed_in
    back_own, both_grads = back_block(own_kept, weights, relaxed_bar, step_size, start_grads)
    corrected = forward[1]
    grad_cpoints = jnp.where(leading, back_own + back_start, back_own)
    grad_weights = dp_sum(both_grads, "dp")
    return (corrected[None], grad_cpoints[None], grad_weights)


def solution(mesh):
    placed = (
        P("depth", "dp", None, None),
        P("depth", None, None),
        P("depth", None),
        P("depth", "dp", None, None),
    )
    return jax.shard_map(
        body,
        mesh=mesh,
        in_specs=placed,
        out_specs=(
            P("depth", "dp", None, None),
            P("depth", "dp", None, None),
            P("depth", None, None),
        ),
        check_vma=False,
    )
```

```python
import functools

import jax
import jax.numpy as jnp
from jax import lax
from jax.sharding import PartitionSpec as P
from jax.experimental import pallas as pl
from jax.experimental.pallas import tpu as pltpu

WID = 16


TAP_OFFSETS = [(-1, -1), (-1, 0), (-1, 1), (0, -1), (0, 0), (0, 1), (1, -1), (1, 0), (1, 1)]


def pack(gains, states):
    width = states.shape[-1]
    rows = [jnp.pad(g, (0, width - g.shape[0]))[None] for g in gains]
    return jnp.concatenate([states.reshape(-1, width)] + rows, axis=0)


def exchange(gains, states, axis, mask):
    count = lax.axis_size(axis)
    arrived = lax.ppermute(pack(gains, states), axis, [(i, i ^ mask) for i in range(count)])
    rows = states.size // states.shape[-1]
    each = states.shape[1:]
    got = arrived[:rows].reshape(states.shape)
    return tuple(
        (arrived[rows + k, : g.shape[0]], got[k].reshape(each)) for k, g in enumerate(gains)
    )


def scan_round(scan, arrived, partner_first, bit, last):
    part_gain, part_state, whole_gain, whole_state = scan
    got_gain, got_state = arrived
    take = partner_first(bit)
    part_state = jnp.where(take, part_state + part_gain[:, None] * got_state, part_state)
    part_gain = jnp.where(take, part_gain * got_gain, part_gain)
    if not last:
        whole_state = jnp.where(
            take,
            whole_state + whole_gain[:, None] * got_state,
            got_state + got_gain[:, None] * whole_state,
        )
        whole_gain = whole_gain * got_gain
    return (part_gain, part_state, whole_gain, whole_state)


def dp_sum(terms, axis):
    count = lax.axis_size(axis)
    if count != terms.shape[0] or count & (count - 1):
        return lax.psum(terms, axis)
    place = lax.axis_index(axis)
    pairs = lambda k: [(i, i ^ k) for i in range(count)]
    got = [terms[place]] + [
        lax.ppermute(lax.dynamic_index_in_dim(terms, place ^ k, 0, False), axis, pairs(k))
        for k in range(1, count)
    ]
    total = got[0]
    for piece in got[1:]:
        total = total + piece
    back = jnp.stack([total] + [lax.ppermute(total, axis, pairs(k)) for k in range(1, count)])
    return jnp.take(back, jnp.arange(count) ^ place, axis=0)


def passed_along(block, axis, distance):
    devices = range(lax.axis_size(axis))
    route = [(i - distance, i) for i in devices if i - distance in devices]
    return lax.ppermute(block, axis, route)


def shift_pixels(values, shift_down, shift_right, row_width):
    pixel_count = values.shape[-1]
    offset = shift_down * row_width + shift_right
    padded = jnp.pad(values, [(0, 0)] * (values.ndim - 1) + [(row_width + 1, row_width + 1)])
    shifted = lax.slice_in_dim(
        padded, row_width + 1 + offset, row_width + 1 + offset + pixel_count, axis=values.ndim - 1
    )
    column = jnp.arange(pixel_count) % row_width + shift_right
    inside = (column >= 0) & (column < row_width)
    return jnp.where(inside, shifted, jnp.zeros_like(shifted))


def unfold(values, row_width):
    return jnp.concatenate([shift_pixels(values, a, b, row_width) for a, b in TAP_OFFSETS], axis=1)


def fold_taps(tap_grads, row_width):
    channels = tap_grads.shape[1] // 9
    accumulated = jnp.zeros((tap_grads.shape[0], channels, tap_grads.shape[2]), jnp.float32)
    for tap_index, (a, b) in enumerate(TAP_OFFSETS):
        piece = tap_grads[:, tap_index * channels : (tap_index + 1) * channels]
        accumulated = accumulated + shift_pixels(piece, -a, -b, row_width)
    return accumulated


def unfold_taps(squashed, row, column):
    pixels = squashed.shape[-1]
    pieces = []
    for down, right in TAP_OFFSETS:
        shift = down * WID + right
        moved = pltpu.roll(squashed, (-shift) % pixels, 1) if shift else squashed
        inside = (row + down >= 0) & (row + down < WID) & (column + right >= 0) & (column + right < WID)
        pieces.append(jnp.where(inside, moved, 0.0).astype(jnp.bfloat16))
    return jnp.concatenate(pieces, axis=0)


def pixel_grid(pixels):
    place = lax.broadcasted_iota(jnp.int32, (1, pixels), 1)
    return place // WID, place % WID


def block_kernel(step_size, state_ref, weight_ref, out_ref, kept_ref):
    current = state_ref[...]
    row, column = pixel_grid(current.shape[-1])
    for layer in range(weight_ref.shape[0]):
        kept_ref[layer] = current
        patches = unfold_taps(jnp.tanh(current), row, column)
        mixed = jnp.dot(weight_ref[layer], patches, preferred_element_type=jnp.float32)
        current = current + step_size * mixed
    out_ref[...] = current


def back_kernel(step_size, kept_ref, flipped_ref, upstream_ref, out_ref, grads_ref):
    upstream = upstream_ref[...]
    channels, pixels = upstream.shape
    row, column = pixel_grid(pixels)
    for layer in reversed(range(kept_ref.shape[0])):
        squashed = jnp.tanh(kept_ref[layer])
        patches = unfold_taps(squashed, row, column)
        scaled = (step_size * upstream).astype(jnp.bfloat16)
        grads_ref[layer] = lax.dot_general(
            scaled, patches, (((1,), (1,)), ((), ())), preferred_element_type=jnp.float32
        )
        spread = jnp.dot(flipped_ref[layer], scaled, preferred_element_type=jnp.float32)
        folded = jnp.zeros((channels, pixels), jnp.float32)
        for tap, (down, right) in enumerate(TAP_OFFSETS):
            shift = down * WID + right
            piece = spread[tap * channels : (tap + 1) * channels]
            moved = pltpu.roll(piece, shift % pixels, 1) if shift else piece
            inside = (row - down >= 0) & (row - down < WID) & (column - right >= 0) & (column - right < WID)
            folded = folded + jnp.where(inside, moved, 0.0)
        upstream = upstream + (1.0 - squashed * squashed) * folded
    out_ref[...] = upstream


def run_block(current, block_weights, step_size):
    layers, channels, pixels = block_weights.shape[0], current.shape[-2], current.shape[-1]
    spec = pl.BlockSpec(memory_space=pltpu.VMEM)
    out, kept = pl.pallas_call(
        functools.partial(block_kernel, step_size),
        out_shape=(
            jax.ShapeDtypeStruct((channels, pixels), jnp.float32),
            jax.ShapeDtypeStruct((layers, channels, pixels), jnp.float32),
        ),
        in_specs=[spec, spec],
        out_specs=(spec, spec),
        cost_estimate=pl.CostEstimate(
            flops=2 * layers * channels * block_weights.shape[-1] * pixels,
            transcendentals=layers * channels * pixels,
            bytes_accessed=4 * (layers + 2) * channels * pixels + 2 * block_weights.size,
        ),
    )(current.reshape(channels, pixels), block_weights)
    return (out.reshape(current.shape), kept)


def back_block(inputs_kept, block_weights, upstream, step_size):
    layers, channels, pixels = block_weights.shape[0], upstream.shape[-2], upstream.shape[-1]
    taps = block_weights.shape[-1]
    flipped = jnp.swapaxes(block_weights, 1, 2)
    spec = pl.BlockSpec(memory_space=pltpu.VMEM)
    out, grads = pl.pallas_call(
        functools.partial(back_kernel, step_size),
        out_shape=(
            jax.ShapeDtypeStruct((channels, pixels), jnp.float32),
            jax.ShapeDtypeStruct((layers, channels, taps), jnp.float32),
        ),
        in_specs=[spec, spec, spec],
        out_specs=(spec, spec),
        cost_estimate=pl.CostEstimate(
            flops=4 * layers * channels * taps * pixels,
            transcendentals=layers * channels * pixels,
            bytes_accessed=4 * (layers + 2) * channels * pixels + 2 * block_weights.size + 4 * layers * channels * taps,
        ),
    )(inputs_kept, flipped, upstream.reshape(channels, pixels))
    return (out.reshape(upstream.shape), grads)


def body(cpoints, weights, coarse_gain, cotangent):
    step_size = 1.0 / (weights.shape[0] * lax.axis_size("depth"))
    rounds = (lax.axis_size("depth") - 1).bit_length()
    place = lax.axis_index("depth")
    own_state = cpoints[0]
    rate_vec = coarse_gain[0]
    cot_here = cotangent[0]
    leading = place == 0

    def before(bit):
        return (place >> bit) % 2 == 1

    def after(bit):
        return (place >> bit) % 2 == 0

    relaxed, own_kept = run_block(own_state, weights, step_size)
    arriving = passed_along(relaxed, "depth", 1)
    start_state = jnp.where(leading, own_state, arriving)
    propagated, start_kept = run_block(start_state, weights, step_size)
    gained_start = rate_vec[None, :, None] * start_state
    offset = propagated - jnp.where(leading, jnp.zeros_like(gained_start), gained_start)
    forward = (rate_vec, offset, rate_vec, offset)
    reverse = (jnp.ones_like(rate_vec), jnp.zeros_like(cot_here), rate_vec, rate_vec[None, :, None] * cot_here)
    for bit in range(rounds):
        wide = {rounds - 1, 2} if rounds >= 4 else {rounds - 1}
        mask = 3 << (bit - 1) if bit in wide and bit >= 1 else 1 << bit
        got_f, got_r = exchange(
            (forward[2], reverse[2]), jnp.stack([forward[3], reverse[3]]), "depth", mask
        )
        forward = scan_round(forward, got_f, before, bit, bit == rounds - 1)
        reverse = scan_round(reverse, got_r, after, bit, bit == rounds - 1)
    passed_in = reverse[1]
    adjoint_here = cot_here + passed_in
    back_start, start_grads = back_block(start_kept, weights, adjoint_here, step_size)
    arriving_bar = passed_along(back_start, "depth", -1)
    relaxed_bar = arriving_bar - passed_in
    back_own, own_grads = back_block(own_kept, weights, relaxed_bar, step_size)
    corrected = forward[1]
    grad_cpoints = jnp.where(leading, back_own + back_start, back_own)
    grad_weights = dp_sum(start_grads + own_grads, "dp")
    return (corrected[None], grad_cpoints[None], grad_weights)


def solution(mesh):
    placed = (
        P("depth", "dp", None, None),
        P("depth", None, None),
        P("depth", None),
        P("depth", "dp", None, None),
    )
    return jax.shard_map(
        body,
        mesh=mesh,
        in_specs=placed,
        out_specs=(
            P("depth", "dp", None, None),
            P("depth", "dp", None, None),
            P("depth", None, None),
        ),
        check_vma=False,
    )
```

```python
import functools

import jax
import jax.numpy as jnp
from jax import lax
from jax.sharding import PartitionSpec as P
from jax.experimental import pallas as pl
from jax.experimental.pallas import tpu as pltpu

WID = 16


TAP_OFFSETS = [(-1, -1), (-1, 0), (-1, 1), (0, -1), (0, 0), (0, 1), (1, -1), (1, 0), (1, 1)]


def pack(gains, states):
    width = states.shape[-1]
    rows = [jnp.pad(g, (0, width - g.shape[0]))[None] for g in gains]
    return jnp.concatenate([states.reshape(-1, width)] + rows, axis=0)


def exchange(gains, states, axis, mask):
    count = lax.axis_size(axis)
    arrived = lax.ppermute(pack(gains, states), axis, [(i, i ^ mask) for i in range(count)])
    rows = states.size // states.shape[-1]
    each = states.shape[1:]
    got = arrived[:rows].reshape(states.shape)
    return tuple(
        (arrived[rows + k, : g.shape[0]], got[k].reshape(each)) for k, g in enumerate(gains)
    )


def scan_round(scan, arrived, partner_first, bit, last):
    part_gain, part_state, whole_gain, whole_state = scan
    got_gain, got_state = arrived
    take = partner_first(bit)
    part_state = jnp.where(take, part_state + part_gain[:, None] * got_state, part_state)
    part_gain = jnp.where(take, part_gain * got_gain, part_gain)
    if not last:
        whole_state = jnp.where(
            take,
            whole_state + whole_gain[:, None] * got_state,
            got_state + got_gain[:, None] * whole_state,
        )
        whole_gain = whole_gain * got_gain
    return (part_gain, part_state, whole_gain, whole_state)


def dp_sum(terms, axis):
    count = lax.axis_size(axis)
    if count != terms.shape[0]:
        return lax.psum(terms, axis)
    got = lax.all_to_all(terms, axis, 0, 0)
    total = got[0]
    for k in range(1, count):
        total = total + got[k]
    return lax.all_to_all(jnp.broadcast_to(total[None], terms.shape), axis, 0, 0)


def passed_along(block, axis, distance):
    devices = range(lax.axis_size(axis))
    route = [(i - distance, i) for i in devices if i - distance in devices]
    return lax.ppermute(block, axis, route)


def shift_pixels(values, shift_down, shift_right, row_width):
    pixel_count = values.shape[-1]
    offset = shift_down * row_width + shift_right
    padded = jnp.pad(values, [(0, 0)] * (values.ndim - 1) + [(row_width + 1, row_width + 1)])
    shifted = lax.slice_in_dim(
        padded, row_width + 1 + offset, row_width + 1 + offset + pixel_count, axis=values.ndim - 1
    )
    column = jnp.arange(pixel_count) % row_width + shift_right
    inside = (column >= 0) & (column < row_width)
    return jnp.where(inside, shifted, jnp.zeros_like(shifted))


def unfold(values, row_width):
    return jnp.concatenate([shift_pixels(values, a, b, row_width) for a, b in TAP_OFFSETS], axis=1)


def fold_taps(tap_grads, row_width):
    channels = tap_grads.shape[1] // 9
    accumulated = jnp.zeros((tap_grads.shape[0], channels, tap_grads.shape[2]), jnp.float32)
    for tap_index, (a, b) in enumerate(TAP_OFFSETS):
        piece = tap_grads[:, tap_index * channels : (tap_index + 1) * channels]
        accumulated = accumulated + shift_pixels(piece, -a, -b, row_width)
    return accumulated


def unfold_taps(squashed, row, column):
    pixels = squashed.shape[-1]
    pieces = []
    for down, right in TAP_OFFSETS:
        shift = down * WID + right
        moved = pltpu.roll(squashed, (-shift) % pixels, 1) if shift else squashed
        inside = (row + down >= 0) & (row + down < WID) & (column + right >= 0) & (column + right < WID)
        pieces.append(jnp.where(inside, moved, 0.0).astype(jnp.bfloat16))
    return jnp.concatenate(pieces, axis=0)


def pixel_grid(pixels):
    place = lax.broadcasted_iota(jnp.int32, (1, pixels), 1)
    return place // WID, place % WID


def block_kernel(step_size, state_ref, weight_ref, out_ref, kept_ref):
    current = state_ref[...]
    row, column = pixel_grid(current.shape[-1])
    for layer in range(weight_ref.shape[0]):
        kept_ref[layer] = current
        patches = unfold_taps(jnp.tanh(current), row, column)
        mixed = jnp.dot(weight_ref[layer], patches, preferred_element_type=jnp.float32)
        current = current + step_size * mixed
    out_ref[...] = current


def back_kernel(step_size, kept_ref, flipped_ref, upstream_ref, out_ref, grads_ref):
    upstream = upstream_ref[...]
    channels, pixels = upstream.shape
    row, column = pixel_grid(pixels)
    for layer in reversed(range(kept_ref.shape[0])):
        squashed = jnp.tanh(kept_ref[layer])
        patches = unfold_taps(squashed, row, column)
        scaled = (step_size * upstream).astype(jnp.bfloat16)
        grads_ref[layer] = lax.dot_general(
            scaled, patches, (((1,), (1,)), ((), ())), preferred_element_type=jnp.float32
        )
        spread = jnp.dot(flipped_ref[layer], scaled, preferred_element_type=jnp.float32)
        folded = jnp.zeros((channels, pixels), jnp.float32)
        for tap, (down, right) in enumerate(TAP_OFFSETS):
            shift = down * WID + right
            piece = spread[tap * channels : (tap + 1) * channels]
            moved = pltpu.roll(piece, shift % pixels, 1) if shift else piece
            inside = (row - down >= 0) & (row - down < WID) & (column - right >= 0) & (column - right < WID)
            folded = folded + jnp.where(inside, moved, 0.0)
        upstream = upstream + (1.0 - squashed * squashed) * folded
    out_ref[...] = upstream


def run_block(current, block_weights, step_size):
    layers, channels, pixels = block_weights.shape[0], current.shape[-2], current.shape[-1]
    spec = pl.BlockSpec(memory_space=pltpu.VMEM)
    out, kept = pl.pallas_call(
        functools.partial(block_kernel, step_size),
        out_shape=(
            jax.ShapeDtypeStruct((channels, pixels), jnp.float32),
            jax.ShapeDtypeStruct((layers, channels, pixels), jnp.float32),
        ),
        in_specs=[spec, spec],
        out_specs=(spec, spec),
        cost_estimate=pl.CostEstimate(
            flops=2 * layers * channels * block_weights.shape[-1] * pixels,
            transcendentals=layers * channels * pixels,
            bytes_accessed=4 * (layers + 2) * channels * pixels + 2 * block_weights.size,
        ),
    )(current.reshape(channels, pixels), block_weights)
    return (out.reshape(current.shape), kept)


def back_block(inputs_kept, block_weights, upstream, step_size):
    layers, channels, pixels = block_weights.shape[0], upstream.shape[-2], upstream.shape[-1]
    taps = block_weights.shape[-1]
    flipped = jnp.swapaxes(block_weights, 1, 2)
    spec = pl.BlockSpec(memory_space=pltpu.VMEM)
    out, grads = pl.pallas_call(
        functools.partial(back_kernel, step_size),
        out_shape=(
            jax.ShapeDtypeStruct((channels, pixels), jnp.float32),
            jax.ShapeDtypeStruct((layers, channels, taps), jnp.float32),
        ),
        in_specs=[spec, spec, spec],
        out_specs=(spec, spec),
        cost_estimate=pl.CostEstimate(
            flops=4 * layers * channels * taps * pixels,
            transcendentals=layers * channels * pixels,
            bytes_accessed=4 * (layers + 2) * channels * pixels + 2 * block_weights.size + 4 * layers * channels * taps,
        ),
    )(inputs_kept, flipped, upstream.reshape(channels, pixels))
    return (out.reshape(upstream.shape), grads)


def body(cpoints, weights, coarse_gain, cotangent):
    step_size = 1.0 / (weights.shape[0] * lax.axis_size("depth"))
    rounds = (lax.axis_size("depth") - 1).bit_length()
    place = lax.axis_index("depth")
    own_state = cpoints[0]
    rate_vec = coarse_gain[0]
    cot_here = cotangent[0]
    leading = place == 0

    def before(bit):
        return (place >> bit) % 2 == 1

    def after(bit):
        return (place >> bit) % 2 == 0

    relaxed, own_kept = run_block(own_state, weights, step_size)
    arriving = passed_along(relaxed, "depth", 1)
    start_state = jnp.where(leading, own_state, arriving)
    propagated, start_kept = run_block(start_state, weights, step_size)
    gained_start = rate_vec[None, :, None] * start_state
    offset = propagated - jnp.where(leading, jnp.zeros_like(gained_start), gained_start)
    forward = (rate_vec, offset, rate_vec, offset)
    reverse = (jnp.ones_like(rate_vec), jnp.zeros_like(cot_here), rate_vec, rate_vec[None, :, None] * cot_here)
    for bit in range(rounds):
        wide = {rounds - 1, 2} if rounds >= 4 else {rounds - 1}
        mask = 3 << (bit - 1) if bit in wide and bit >= 1 else 1 << bit
        got_f, got_r = exchange(
            (forward[2], reverse[2]), jnp.stack([forward[3], reverse[3]]), "depth", mask
        )
        forward = scan_round(forward, got_f, before, bit, bit == rounds - 1)
        reverse = scan_round(reverse, got_r, after, bit, bit == rounds - 1)
    passed_in = reverse[1]
    adjoint_here = cot_here + passed_in
    back_start, start_grads = back_block(start_kept, weights, adjoint_here, step_size)
    arriving_bar = passed_along(back_start, "depth", -1)
    relaxed_bar = arriving_bar - passed_in
    back_own, own_grads = back_block(own_kept, weights, relaxed_bar, step_size)
    corrected = forward[1]
    grad_cpoints = jnp.where(leading, back_own + back_start, back_own)
    grad_weights = dp_sum(start_grads + own_grads, "dp")
    return (corrected[None], grad_cpoints[None], grad_weights)


def solution(mesh):
    placed = (
        P("depth", "dp", None, None),
        P("depth", None, None),
        P("depth", None),
        P("depth", "dp", None, None),
    )
    return jax.shard_map(
        body,
        mesh=mesh,
        in_specs=placed,
        out_specs=(
            P("depth", "dp", None, None),
            P("depth", "dp", None, None),
            P("depth", None, None),
        ),
        check_vma=False,
    )
```
